128 devices in a mesh: dom: 8 (over x, core), band: 16 (over z, y).
Axes of the slice: x: 4, y: 4, z: 4, core: 2. Of those that a mesh axis runs over, the one named last changes fastest.
Arguments:
- psi: float32 [192, 32, 32, 128], P('band', 'dom'), may hold values from -6 to 6
- potential: float32 [32, 32, 128], P('dom'), may hold values from -3 to 0
Outputs:
- basis: float32 [192, 32, 32, 128], P('band', 'dom')
- projected: float32 [192, 192], P('band')
The draws below stay inside these ranges and needn't reach their ends.
All inputs are finite; a program needn't handle non-finite values.
Results may differ from the reference program's by a relative error of at most 0.000092.
Values sent between devices are 32-bit elements; how exact they have to be, the bound alone decides.
No kernel may reach another device: no remote copies, remote signals or barrier semaphores. Data moves between devices by JAX's collectives and lax.ppermute only.
A program may use at most 128 MiB of HBM per device.

```python
import jax
import jax.numpy as jnp
from jax import lax

BANDS = 192
DEGREE = 4
NX = 128
NY = 32
NZ = 32


def steps_of(stream_key, extent, split, smallest, high):
    factor_of, own = 1.0, jax.random.fold_in(stream_key, 6)
    for axis_at, blocks in split:
        steps = jnp.exp(jax.random.uniform(jax.random.fold_in(own, axis_at), (blocks,), jnp.float32, smallest / len(split), high / len(split)))
        factor_of = factor_of * jnp.repeat(steps, extent[axis_at] // blocks).reshape([-1 if axis == axis_at else 1 for axis in range(len(extent))])
    return factor_of


def noise(stream_key, shape, scale, most, split=(), kind=jnp.bfloat16):
    entries = jax.random.normal(stream_key, shape, jnp.float32) * scale
    if len(split) > 0:
        entries = steps_of(stream_key, shape, split, -0.22, 0.18) * entries
    return jnp.clip(entries, min=-most, max=most).astype(kind)


def setup_inputs(seed: int = 0) -> dict:
    key_list = jax.random.split(jax.random.key(seed), 3)
    return {
        "psi": noise(key_list[0], (BANDS, NZ, NY, NX), 1.0, 6.0, ((0, 16), (1, 8)), jnp.float32),
        "potential": jnp.clip(-3.0 + 3.0 * jax.random.uniform(key_list[1], (NZ, NY, NX), jnp.float32) ** steps_of(key_list[1], (NZ, NY, NX), ((0, 8),), -0.2, 0.2), -3.0, 0.0),
    }


stencil_coef = (-205.0 / 72.0, 8.0 / 5.0, -1.0 / 5.0, 8.0 / 315.0, -1.0 / 560.0)
center = 5.25
half = 4.75

def inner(left, right):
    return lax.dot_general(left.astype(jnp.float32), right.astype(jnp.float32), (((1,), (1,)), ((), ())), precision=lax.Precision.HIGHEST, preferred_element_type=jnp.float32)

def hamiltonian(field, potential):
    laplace = 3.0 * stencil_coef[0] * field
    for reach in range(1, 5):
        near = jnp.roll(field, reach, 1) + jnp.roll(field, -reach, 1)
        near = near + jnp.roll(field, reach, 2) + jnp.roll(field, -reach, 2)
        near = near + jnp.roll(field, reach, 3) + jnp.roll(field, -reach, 3)
        laplace = laplace + stencil_coef[reach] * near
    return potential[None] * field - 0.5 * laplace

def reference(psi, potential):
    previous = psi
    current = (hamiltonian(psi, potential) - center * psi) / half
    for order in range(1, DEGREE):
        following = 2.0 / half * (hamiltonian(current, potential) - center * current) - previous
        previous, current = (current, following)
    ncells = NX * NY * NZ
    flat = current.reshape(BANDS, -1)
    correlation = inner(flat, flat) / ncells
    lower = jnp.linalg.cholesky(correlation)
    inverse = jax.scipy.linalg.solve_triangular(lower, jnp.eye(BANDS, dtype=jnp.float32), lower=True)
    basis_flat = jnp.dot(inverse.astype(jnp.float32), flat.astype(jnp.float32), precision=lax.Precision.HIGHEST, preferred_element_type=jnp.float32)
    basis = basis_flat.reshape(psi.shape)
    applied = hamiltonian(basis, potential).reshape(BANDS, -1)
    projected = inner(basis_flat, applied) / ncells
    return (basis, projected)
```

```python
import jax
import jax.numpy as jnp
from jax import lax
from jax.sharding import PartitionSpec as P

DEGREE = 4


stencil_coef = (-205.0 / 72.0, 8.0 / 5.0, -1.0 / 5.0, 8.0 / 315.0, -1.0 / 560.0)
stencil_reach = 4
center = 5.25
half = 4.75


def extended(array, sides, width):
    for axis, dim in sides:
        count, length = (lax.axis_size(axis), array.shape[dim])
        up = [(i, (i + 1) % count) for i in range(count)]
        down = [(j, i) for i, j in up]
        last = lax.slice_in_dim(array, length - width, length, axis=dim)
        initial = lax.slice_in_dim(array, 0, width, axis=dim)
        before = lax.ppermute(last, axis, up)
        after = lax.ppermute(initial, axis, down)
        array = jnp.concatenate([before, array, after], axis=dim)
    return array


def hp_dot(left, right, dims):
    return lax.dot_general(
        left,
        right,
        (dims, ((), ())),
        precision=lax.Precision.HIGHEST,
        preferred_element_type=jnp.float32,
    )


def hamiltonian(field, padded, potential):
    depth = field.shape[1]
    laplace = 3.0 * stencil_coef[0] * field
    for reach in range(1, 5):
        near = (
            padded[:, stencil_reach + reach : stencil_reach + reach + depth]
            + padded[:, stencil_reach - reach : stencil_reach - reach + depth]
        )
        near = near + jnp.roll(field, reach, 2) + jnp.roll(field, -reach, 2)
        near = near + jnp.roll(field, reach, 3) + jnp.roll(field, -reach, 3)
        laplace = laplace + stencil_coef[reach] * near
    return potential[None] * field - 0.5 * laplace


def butterfly_sum(x, axes):
    for axis in axes:
        count = lax.axis_size(axis)
        step = 1
        while step < count:
            pairs = [(i, i ^ step) for i in range(count)]
            x = x + lax.ppermute(x, axis, pairs)
            step *= 2
    return x


def local(psi, potential):
    bdev = psi.shape[0]
    depth, rows_y, rows_x = (psi.shape[1], psi.shape[2], psi.shape[3])
    nbands = bdev * lax.axis_size("band")
    ncells = depth * lax.axis_size("dom") * rows_y * rows_x
    own_start = lax.axis_index("band") * bdev

    def apply(field):
        padded = extended(field, (("dom", 1),), stencil_reach)
        return hamiltonian(field, padded, potential)

    previous = psi
    current = (apply(psi) - center * psi) / half
    for order in range(1, DEGREE):
        following = 2.0 / half * (apply(current) - center * current) - previous
        previous, current = (current, following)
    image = apply(current)
    pair = jnp.stack([current.reshape(bdev, -1), image.reshape(bdev, -1)])
    spread = lax.all_to_all(pair, "band", 2, 1, tiled=True)
    flat_cd, image_cd = spread[0], spread[1]
    sums = jnp.stack(
        [
            hp_dot(flat_cd, flat_cd, ((1,), (1,))),
            hp_dot(flat_cd, image_cd, ((1,), (1,))),
        ]
    )
    sums = butterfly_sum(sums, ("dom", "band")) / ncells
    correlation, gram = sums[0], sums[1]
    lower = jnp.linalg.cholesky(correlation)
    inverse = jax.scipy.linalg.solve_triangular(
        lower, jnp.eye(nbands, dtype=jnp.float32), lower=True
    )
    basis_cd = hp_dot(inverse, flat_cd, ((1,), (0,)))
    basis = lax.all_to_all(basis_cd, "band", 0, 1, tiled=True).reshape(psi.shape)
    own_rows = lax.dynamic_slice_in_dim(inverse, own_start, bdev, 0)
    projected = hp_dot(hp_dot(own_rows, gram, ((1,), (0,))), inverse, ((1,), (1,)))
    return (basis, projected)


def solution(mesh):
    in_specs = (P("band", "dom", None, None), P("dom", None, None))
    out_specs = (P("band", "dom", None, None), P("band", None))
    return jax.shard_map(local, mesh=mesh, in_specs=in_specs, out_specs=out_specs, check_vma=False)
```

```python
import jax
import jax.numpy as jnp
from jax import lax
from jax.experimental import pallas as pl
from jax.experimental.pallas import tpu as pltpu
from jax.sharding import PartitionSpec as P

DEGREE = 4


stencil_coef = (-205.0 / 72.0, 8.0 / 5.0, -1.0 / 5.0, 8.0 / 315.0, -1.0 / 560.0)
stencil_reach = 4
center = 5.25
half = 4.75


def extended(array, sides, width):
    for axis, dim in sides:
        count, length = (lax.axis_size(axis), array.shape[dim])
        up = [(i, (i + 1) % count) for i in range(count)]
        down = [(j, i) for i, j in up]
        last = lax.slice_in_dim(array, length - width, length, axis=dim)
        initial = lax.slice_in_dim(array, 0, width, axis=dim)
        before = lax.ppermute(last, axis, up)
        after = lax.ppermute(initial, axis, down)
        array = jnp.concatenate([before, array, after], axis=dim)
    return array


def hp_dot(left, right, dims):
    return lax.dot_general(
        left,
        right,
        (dims, ((), ())),
        precision=lax.Precision.HIGHEST,
        preferred_element_type=jnp.float32,
    )


def hamiltonian(field, padded, potential):
    depth = field.shape[1]
    laplace = 3.0 * stencil_coef[0] * field
    for reach in range(1, 5):
        near = (
            padded[:, stencil_reach + reach : stencil_reach + reach + depth]
            + padded[:, stencil_reach - reach : stencil_reach - reach + depth]
        )
        near = near + jnp.roll(field, reach, 2) + jnp.roll(field, -reach, 2)
        near = near + jnp.roll(field, reach, 3) + jnp.roll(field, -reach, 3)
        laplace = laplace + stencil_coef[reach] * near
    return potential[None] * field - 0.5 * laplace


def butterfly_sum(x, axes):
    for axis in axes:
        count = lax.axis_size(axis)
        step = 1
        while step < count:
            pairs = [(i, i ^ step) for i in range(count)]
            x = x + lax.ppermute(x, axis, pairs)
            step *= 2
    return x


def gram_kernel(rows, f_ref, h_ref, c_ref, g_ref):
    nb = c_ref.shape[0]
    c_ref[...] = jnp.zeros_like(c_ref)
    g_ref[...] = jnp.zeros_like(g_ref)
    for r in range(rows):
        f = f_ref[pl.ds(r, nb, stride=rows), :]
        h = h_ref[pl.ds(r, nb, stride=rows), :]
        c_ref[...] += hp_dot(f, f, ((1,), (1,)))
        g_ref[...] += hp_dot(f, h, ((1,), (1,)))


def rotate_kernel(rows, m_ref, f_ref, o_ref):
    nb = m_ref.shape[0]
    for r in range(rows):
        o_ref[pl.ds(r, nb, stride=rows), :] = hp_dot(
            m_ref[...], f_ref[pl.ds(r, nb, stride=rows), :], ((1,), (0,))
        )


def vspec():
    return pl.BlockSpec(memory_space=pltpu.VMEM)


def grams(rows, f, h):
    nb = f.shape[0] // rows
    out = jax.ShapeDtypeStruct((nb, nb), jnp.float32)
    return pl.pallas_call(
        lambda *refs: gram_kernel(rows, *refs),
        out_shape=(out, out),
        in_specs=[vspec(), vspec()],
        out_specs=(vspec(), vspec()),
    )(f, h)


def rotate(rows, m, f):
    return pl.pallas_call(
        lambda *refs: rotate_kernel(rows, *refs),
        out_shape=jax.ShapeDtypeStruct(f.shape, jnp.float32),
        in_specs=[vspec(), vspec()],
        out_specs=vspec(),
    )(m, f)


def local(psi, potential):
    bdev = psi.shape[0]
    depth, rows_y, rows_x = (psi.shape[1], psi.shape[2], psi.shape[3])
    nbands = bdev * lax.axis_size("band")
    ncells = depth * lax.axis_size("dom") * rows_y * rows_x
    own_start = lax.axis_index("band") * bdev

    def apply(field):
        padded = extended(field, (("dom", 1),), stencil_reach)
        return hamiltonian(field, padded, potential)

    previous = psi
    current = (apply(psi) - center * psi) / half
    for order in range(1, DEGREE):
        following = 2.0 / half * (apply(current) - center * current) - previous
        previous, current = (current, following)
    image = apply(current)
    groups = lax.axis_size("band")
    rows = depth * rows_y * rows_x // groups // rows_x
    lanes = rows_x
    chunked = jnp.stack([current, image]).reshape(2, bdev, groups, rows, lanes)
    spread = lax.all_to_all(chunked, "band", 2, 2, tiled=True)
    flat_cd = spread[0].reshape(bdev * groups * rows, lanes)
    image_cd = spread[1].reshape(bdev * groups * rows, lanes)
    c_perm, g_perm = grams(rows, flat_cd, image_cd)
    sums = butterfly_sum(jnp.stack([c_perm, g_perm]), ("dom", "band")) / ncells

    def to_true(m):
        return m.reshape(bdev, groups, bdev, groups).transpose(1, 0, 3, 2).reshape(nbands, nbands)

    def to_perm(m):
        return m.reshape(groups, bdev, groups, bdev).transpose(1, 0, 3, 2).reshape(nbands, nbands)

    correlation, gram = to_true(sums[0]), to_true(sums[1])
    lower = jnp.linalg.cholesky(correlation)
    inverse = jax.scipy.linalg.solve_triangular(
        lower, jnp.eye(nbands, dtype=jnp.float32), lower=True
    )
    basis_cd = rotate(rows, to_perm(inverse), flat_cd).reshape(bdev, groups, rows, lanes)
    basis = lax.all_to_all(basis_cd, "band", 1, 1, tiled=True).reshape(psi.shape)
    own_rows = lax.dynamic_slice_in_dim(inverse, own_start, bdev, 0)
    projected = hp_dot(hp_dot(own_rows, gram, ((1,), (0,))), inverse, ((1,), (1,)))
    return (basis, projected)


def solution(mesh):
    in_specs = (P("band", "dom", None, None), P("dom", None, None))
    out_specs = (P("band", "dom", None, None), P("band", None))
    return jax.shard_map(local, mesh=mesh, in_specs=in_specs, out_specs=out_specs, check_vma=False)
```

```python
import jax
import jax.numpy as jnp
from jax import lax
from jax.experimental import pallas as pl
from jax.experimental.pallas import tpu as pltpu
from jax.sharding import PartitionSpec as P

DEGREE = 4


stencil_coef = (-205.0 / 72.0, 8.0 / 5.0, -1.0 / 5.0, 8.0 / 315.0, -1.0 / 560.0)
stencil_reach = 4
center = 5.25
half = 4.75


def extended(array, sides, width):
    for axis, dim in sides:
        count, length = (lax.axis_size(axis), array.shape[dim])
        up = [(i, (i + 1) % count) for i in range(count)]
        down = [(j, i) for i, j in up]
        last = lax.slice_in_dim(array, length - width, length, axis=dim)
        initial = lax.slice_in_dim(array, 0, width, axis=dim)
        before = lax.ppermute(last, axis, up)
        after = lax.ppermute(initial, axis, down)
        array = jnp.concatenate([before, array, after], axis=dim)
    return array


def hp_dot(left, right, dims):
    return lax.dot_general(
        left,
        right,
        (dims, ((), ())),
        precision=lax.Precision.HIGHEST,
        preferred_element_type=jnp.float32,
    )


def hamiltonian(field, padded, potential):
    depth = field.shape[1]
    laplace = 3.0 * stencil_coef[0] * field
    for reach in range(1, 5):
        near = (
            padded[:, stencil_reach + reach : stencil_reach + reach + depth]
            + padded[:, stencil_reach - reach : stencil_reach - reach + depth]
        )
        near = near + jnp.roll(field, reach, 2) + jnp.roll(field, -reach, 2)
        near = near + jnp.roll(field, reach, 3) + jnp.roll(field, -reach, 3)
        laplace = laplace + stencil_coef[reach] * near
    return potential[None] * field - 0.5 * laplace


def group_sum(x, axis, stride, size):
    count = lax.axis_size(axis)
    pos = (lax.axis_index(axis) // stride) % size
    received = [x]
    for shift in range(1, size):
        pairs = []
        for i in range(count):
            p = (i // stride) % size
            pairs.append((i, i + (((p + shift) % size) - p) * stride))
        received.append(lax.ppermute(x, axis, pairs))
    def at(p):
        value = received[0]
        for shift in range(1, size):
            value = jnp.where((pos - p) % size == shift, received[shift], value)
        return value
    values = [at(p) for p in range(size)]
    while len(values) > 1:
        values = [values[i] + values[i + 1] for i in range(0, len(values), 2)]
    return values[0]


def mesh_sum(x):
    x = group_sum(x, "dom", 1, 2)
    x = group_sum(x, "dom", 2, lax.axis_size("dom") // 2)
    x = group_sum(x, "band", 1, 4)
    return group_sum(x, "band", 4, lax.axis_size("band") // 4)


def gram_kernel(rows, f_ref, h_ref, c_ref, g_ref):
    nb = c_ref.shape[0]
    c_ref[...] = jnp.zeros_like(c_ref)
    g_ref[...] = jnp.zeros_like(g_ref)
    for r in range(rows):
        f = f_ref[pl.ds(r, nb, stride=rows), :]
        h = h_ref[pl.ds(r, nb, stride=rows), :]
        c_ref[...] += hp_dot(f, f, ((1,), (1,)))
        g_ref[...] += hp_dot(f, h, ((1,), (1,)))


def rotate_kernel(rows, m_ref, f_ref, o_ref):
    nb = m_ref.shape[0]
    for r in range(rows):
        o_ref[pl.ds(r, nb, stride=rows), :] = hp_dot(
            m_ref[...], f_ref[pl.ds(r, nb, stride=rows), :], ((1,), (0,))
        )


def vspec():
    return pl.BlockSpec(memory_space=pltpu.VMEM)


def grams(rows, f, h):
    nb = f.shape[0] // rows
    out = jax.ShapeDtypeStruct((nb, nb), jnp.float32)
    return pl.pallas_call(
        lambda *refs: gram_kernel(rows, *refs),
        out_shape=(out, out),
        in_specs=[vspec(), vspec()],
        out_specs=(vspec(), vspec()),
    )(f, h)


def rotate(rows, m, f):
    return pl.pallas_call(
        lambda *refs: rotate_kernel(rows, *refs),
        out_shape=jax.ShapeDtypeStruct(f.shape, jnp.float32),
        in_specs=[vspec(), vspec()],
        out_specs=vspec(),
    )(m, f)


def local(psi, potential):
    bdev = psi.shape[0]
    depth, rows_y, rows_x = (psi.shape[1], psi.shape[2], psi.shape[3])
    nbands = bdev * lax.axis_size("band")
    ncells = depth * lax.axis_size("dom") * rows_y * rows_x
    own_start = lax.axis_index("band") * bdev

    def apply(field):
        padded = extended(field, (("dom", 1),), stencil_reach)
        return hamiltonian(field, padded, potential)

    previous = psi
    current = (apply(psi) - center * psi) / half
    for order in range(1, DEGREE):
        following = 2.0 / half * (apply(current) - center * current) - previous
        previous, current = (current, following)
    image = apply(current)
    groups = lax.axis_size("band")
    rows = depth * rows_y * rows_x // groups // rows_x
    lanes = rows_x
    chunked = jnp.stack([current, image]).reshape(2, bdev, groups, rows, lanes)
    spread = lax.all_to_all(chunked, "band", 2, 2, tiled=True)
    flat_cd = spread[0].reshape(bdev * groups * rows, lanes)
    image_cd = spread[1].reshape(bdev * groups * rows, lanes)
    c_perm, g_perm = grams(rows, flat_cd, image_cd)
    below = lax.broadcasted_iota(jnp.int32, (nbands, nbands), 0) >= lax.broadcasted_iota(
        jnp.int32, (nbands, nbands), 1
    )
    packed = jnp.concatenate(
        [jnp.where(below, c_perm, g_perm), jnp.diagonal(g_perm)[None], jnp.zeros((7, nbands), jnp.float32)]
    )
    packed = mesh_sum(packed) / ncells
    tri, g_diag = packed[:nbands], packed[nbands]
    c_sum = jnp.where(below, tri, tri.T)
    g_sum = jnp.where(below, tri.T, tri)
    g_sum = jnp.where(jnp.eye(nbands, dtype=bool), g_diag[None, :], g_sum)

    def to_true(m):
        return m.reshape(bdev, groups, bdev, groups).transpose(1, 0, 3, 2).reshape(nbands, nbands)

    def to_perm(m):
        return m.reshape(groups, bdev, groups, bdev).transpose(1, 0, 3, 2).reshape(nbands, nbands)

    correlation, gram = to_true(c_sum), to_true(g_sum)
    lower = jnp.linalg.cholesky(correlation)
    inverse = jax.scipy.linalg.solve_triangular(
        lower, jnp.eye(nbands, dtype=jnp.float32), lower=True
    )
    basis_cd = rotate(rows, to_perm(inverse), flat_cd).reshape(bdev, groups, rows, lanes)
    basis = lax.all_to_all(basis_cd, "band", 1, 1, tiled=True).reshape(psi.shape)
    own_rows = lax.dynamic_slice_in_dim(inverse, own_start, bdev, 0)
    projected = hp_dot(hp_dot(own_rows, gram, ((1,), (0,))), inverse, ((1,), (1,)))
    return (basis, projected)


def solution(mesh):
    in_specs = (P("band", "dom", None, None), P("dom", None, None))
    out_specs = (P("band", "dom", None, None), P("band", None))
    return jax.shard_map(local, mesh=mesh, in_specs=in_specs, out_specs=out_specs, check_vma=False)
```

```python
import jax
import jax.numpy as jnp
from jax import lax
from jax.experimental import pallas as pl
from jax.experimental.pallas import tpu as pltpu
from jax.sharding import PartitionSpec as P

DEGREE = 4


stencil_coef = (-205.0 / 72.0, 8.0 / 5.0, -1.0 / 5.0, 8.0 / 315.0, -1.0 / 560.0)
stencil_reach = 4
center = 5.25
half = 4.75


def extended(array, sides, width):
    for axis, dim in sides:
        count, length = (lax.axis_size(axis), array.shape[dim])
        up = [(i, (i + 1) % count) for i in range(count)]
        down = [(j, i) for i, j in up]
        last = lax.slice_in_dim(array, length - width, length, axis=dim)
        initial = lax.slice_in_dim(array, 0, width, axis=dim)
        before = lax.ppermute(last, axis, up)
        after = lax.ppermute(initial, axis, down)
        array = jnp.concatenate([before, array, after], axis=dim)
    return array


def hp_dot(left, right, dims):
    return lax.dot_general(
        left,
        right,
        (dims, ((), ())),
        precision=lax.Precision.HIGHEST,
        preferred_element_type=jnp.float32,
    )


def hamiltonian(field, padded, potential):
    depth = field.shape[1]
    laplace = 3.0 * stencil_coef[0] * field
    for reach in range(1, 5):
        near = (
            padded[:, stencil_reach + reach : stencil_reach + reach + depth]
            + padded[:, stencil_reach - reach : stencil_reach - reach + depth]
        )
        near = near + jnp.roll(field, reach, 2) + jnp.roll(field, -reach, 2)
        near = near + jnp.roll(field, reach, 3) + jnp.roll(field, -reach, 3)
        laplace = laplace + stencil_coef[reach] * near
    return potential[None] * field - 0.5 * laplace


def group_sum(x, axis, stride, size):
    count = lax.axis_size(axis)
    pos = (lax.axis_index(axis) // stride) % size
    received = [x]
    for shift in range(1, size):
        pairs = []
        for i in range(count):
            p = (i // stride) % size
            pairs.append((i, i + (((p + shift) % size) - p) * stride))
        received.append(lax.ppermute(x, axis, pairs))
    def at(p):
        value = received[0]
        for shift in range(1, size):
            value = jnp.where((pos - p) % size == shift, received[shift], value)
        return value
    values = [at(p) for p in range(size)]
    while len(values) > 1:
        values = [values[i] + values[i + 1] for i in range(0, len(values), 2)]
    return values[0]


def mesh_sum(x):
    x = group_sum(x, "dom", 1, 2)
    x = group_sum(x, "dom", 2, lax.axis_size("dom") // 2)
    x = group_sum(x, "band", 1, 4)
    return group_sum(x, "band", 4, lax.axis_size("band") // 4)


def gram_kernel(rows, f_ref, h_ref, c_ref, g_ref):
    nb = c_ref.shape[0]
    c_ref[...] = jnp.zeros_like(c_ref)
    g_ref[...] = jnp.zeros_like(g_ref)
    for r in range(rows):
        f = f_ref[pl.ds(r, nb, stride=rows), :]
        h = h_ref[pl.ds(r, nb, stride=rows), :]
        c_ref[...] += hp_dot(f, f, ((1,), (1,)))
        g_ref[...] += hp_dot(f, h, ((1,), (1,)))


def rotate_kernel(rows, m_ref, f_ref, o_ref):
    nb = m_ref.shape[0]
    for r in range(rows):
        o_ref[pl.ds(r, nb, stride=rows), :] = hp_dot(
            m_ref[...], f_ref[pl.ds(r, nb, stride=rows), :], ((1,), (0,))
        )


def inverse_kernel(c_ref, o_ref, a_ref, b_ref):
    n = c_ref.shape[0]
    a_ref[...] = jnp.zeros_like(a_ref)
    a_ref[:, :n] = c_ref[...]
    shape = a_ref.shape
    sub = lax.broadcasted_iota(jnp.int32, shape, 0)
    lane = lax.broadcasted_iota(jnp.int32, shape, 1)
    b_ref[...] = jnp.where(sub == lane, 1.0, 0.0).astype(jnp.float32)

    def step(k, carry):
        row_a = a_ref[pl.ds(k, 1), :]
        row_b = b_ref[pl.ds(k, 1), :]
        a = a_ref[...]
        pivot = jnp.sum(jnp.where(lane[:1] == k, row_a, 0.0), axis=1, keepdims=True)
        col = jnp.sum(jnp.where(lane == k, a, 0.0), axis=1, keepdims=True)
        factor = jnp.where(sub[:, :1] > k, col, 0.0) / pivot
        a_ref[...] = a - factor * row_a
        b_ref[...] = b_ref[...] - factor * row_b
        return carry

    lax.fori_loop(0, n, step, 0)
    a = a_ref[...]
    diag = jnp.sum(jnp.where(sub == lane, a, 0.0), axis=1, keepdims=True)
    o_ref[...] = (b_ref[...] / jnp.sqrt(diag))[:, :n]


def lower_inverse(c):
    n = c.shape[0]
    wide = ((n + 127) // 128) * 128
    return pl.pallas_call(
        inverse_kernel,
        out_shape=jax.ShapeDtypeStruct((n, n), jnp.float32),
        in_specs=[vspec()],
        out_specs=vspec(),
        scratch_shapes=[pltpu.VMEM((n, wide), jnp.float32), pltpu.VMEM((n, wide), jnp.float32)],
    )(c)


def vspec():
    return pl.BlockSpec(memory_space=pltpu.VMEM)


def grams(rows, f, h):
    nb = f.shape[0] // rows
    out = jax.ShapeDtypeStruct((nb, nb), jnp.float32)
    return pl.pallas_call(
        lambda *refs: gram_kernel(rows, *refs),
        out_shape=(out, out),
        in_specs=[vspec(), vspec()],
        out_specs=(vspec(), vspec()),
    )(f, h)


def rotate(rows, m, f):
    return pl.pallas_call(
        lambda *refs: rotate_kernel(rows, *refs),
        out_shape=jax.ShapeDtypeStruct(f.shape, jnp.float32),
        in_specs=[vspec(), vspec()],
        out_specs=vspec(),
    )(m, f)


def local(psi, potential):
    bdev = psi.shape[0]
    depth, rows_y, rows_x = (psi.shape[1], psi.shape[2], psi.shape[3])
    nbands = bdev * lax.axis_size("band")
    ncells = depth * lax.axis_size("dom") * rows_y * rows_x
    own_start = lax.axis_index("band") * bdev

    def apply(field):
        padded = extended(field, (("dom", 1),), stencil_reach)
        return hamiltonian(field, padded, potential)

    previous = psi
    current = (apply(psi) - center * psi) / half
    for order in range(1, DEGREE):
        following = 2.0 / half * (apply(current) - center * current) - previous
        previous, current = (current, following)
    image = apply(current)
    groups = lax.axis_size("band")
    rows = depth * rows_y * rows_x // groups // rows_x
    lanes = rows_x
    chunked = jnp.stack([current, image]).reshape(2, bdev, groups, rows, lanes)
    spread = lax.all_to_all(chunked, "band", 2, 2, tiled=True)
    flat_cd = spread[0].reshape(bdev * groups * rows, lanes)
    image_cd = spread[1].reshape(bdev * groups * rows, lanes)
    c_perm, g_perm = grams(rows, flat_cd, image_cd)
    below = lax.broadcasted_iota(jnp.int32, (nbands, nbands), 0) >= lax.broadcasted_iota(
        jnp.int32, (nbands, nbands), 1
    )
    packed = jnp.concatenate(
        [jnp.where(below, c_perm, g_perm), jnp.diagonal(g_perm)[None], jnp.zeros((7, nbands), jnp.float32)]
    )
    packed = mesh_sum(packed) / ncells
    tri, g_diag = packed[:nbands], packed[nbands]
    c_sum = jnp.where(below, tri, tri.T)
    g_sum = jnp.where(below, tri.T, tri)
    g_sum = jnp.where(jnp.eye(nbands, dtype=bool), g_diag[None, :], g_sum)

    def to_true(m):
        return m.reshape(bdev, groups, bdev, groups).transpose(1, 0, 3, 2).reshape(nbands, nbands)

    def to_perm(m):
        return m.reshape(groups, bdev, groups, bdev).transpose(1, 0, 3, 2).reshape(nbands, nbands)

    correlation, gram = to_true(c_sum), to_true(g_sum)
    inverse = lower_inverse(correlation)
    basis_cd = rotate(rows, to_perm(inverse), flat_cd).reshape(bdev, groups, rows, lanes)
    basis = lax.all_to_all(basis_cd, "band", 1, 1, tiled=True).reshape(psi.shape)
    own_rows = lax.dynamic_slice_in_dim(inverse, own_start, bdev, 0)
    projected = hp_dot(hp_dot(own_rows, gram, ((1,), (0,))), inverse, ((1,), (1,)))
    return (basis, projected)


def solution(mesh):
    in_specs = (P("band", "dom", None, None), P("dom", None, None))
    out_specs = (P("band", "dom", None, None), P("band", None))
    return jax.shard_map(local, mesh=mesh, in_specs=in_specs, out_specs=out_specs, check_vma=False)
```

```python
import jax
import jax.numpy as jnp
from jax import lax
from jax.experimental import pallas as pl
from jax.experimental.pallas import tpu as pltpu
from jax.sharding import PartitionSpec as P

DEGREE = 4
CHUNKS = 2


stencil_coef = (-205.0 / 72.0, 8.0 / 5.0, -1.0 / 5.0, 8.0 / 315.0, -1.0 / 560.0)
stencil_reach = 4
center = 5.25
half = 4.75


def extended(array, sides, width):
    for axis, dim in sides:
        count, length = (lax.axis_size(axis), array.shape[dim])
        up = [(i, (i + 1) % count) for i in range(count)]
        down = [(j, i) for i, j in up]
        last = lax.slice_in_dim(array, length - width, length, axis=dim)
        initial = lax.slice_in_dim(array, 0, width, axis=dim)
        before = lax.ppermute(last, axis, up)
        after = lax.ppermute(initial, axis, down)
        array = jnp.concatenate([before, array, after], axis=dim)
    return array


def hp_dot(left, right, dims):
    return lax.dot_general(
        left,
        right,
        (dims, ((), ())),
        precision=lax.Precision.HIGHEST,
        preferred_element_type=jnp.float32,
    )


def hamiltonian(field, padded, potential):
    depth = field.shape[1]
    laplace = 3.0 * stencil_coef[0] * field
    for reach in range(1, 5):
        near = (
            padded[:, stencil_reach + reach : stencil_reach + reach + depth]
            + padded[:, stencil_reach - reach : stencil_reach - reach + depth]
        )
        near = near + jnp.roll(field, reach, 2) + jnp.roll(field, -reach, 2)
        near = near + jnp.roll(field, reach, 3) + jnp.roll(field, -reach, 3)
        laplace = laplace + stencil_coef[reach] * near
    return potential[None] * field - 0.5 * laplace


def group_sum(x, axis, stride, size):
    count = lax.axis_size(axis)
    pos = (lax.axis_index(axis) // stride) % size
    received = [x]
    for shift in range(1, size):
        pairs = []
        for i in range(count):
            p = (i // stride) % size
            pairs.append((i, i + (((p + shift) % size) - p) * stride))
        received.append(lax.ppermute(x, axis, pairs))
    def at(p):
        value = received[0]
        for shift in range(1, size):
            value = jnp.where((pos - p) % size == shift, received[shift], value)
        return value
    values = [at(p) for p in range(size)]
    while len(values) > 1:
        values = [values[i] + values[i + 1] for i in range(0, len(values), 2)]
    return values[0]


def mesh_sum(x):
    x = group_sum(x, "dom", 1, 2)
    x = group_sum(x, "dom", 2, lax.axis_size("dom") // 2)
    x = group_sum(x, "band", 1, 4)
    return group_sum(x, "band", 4, lax.axis_size("band") // 4)


def gram_kernel(rows, f_ref, h_ref, c_ref, g_ref):
    nb = c_ref.shape[0]
    c_ref[...] = jnp.zeros_like(c_ref)
    g_ref[...] = jnp.zeros_like(g_ref)
    for r in range(rows):
        f = f_ref[pl.ds(r, nb, stride=rows), :]
        h = h_ref[pl.ds(r, nb, stride=rows), :]
        c_ref[...] += hp_dot(f, f, ((1,), (1,)))
        g_ref[...] += hp_dot(f, h, ((1,), (1,)))


def rotate_kernel(rows, m_ref, f_ref, o_ref):
    nb = m_ref.shape[0]
    for r in range(rows):
        o_ref[pl.ds(r, nb, stride=rows), :] = hp_dot(
            m_ref[...], f_ref[pl.ds(r, nb, stride=rows), :], ((1,), (0,))
        )


def inverse_kernel(c_ref, o_ref, a_ref, b_ref):
    n = c_ref.shape[0]
    a_ref[...] = jnp.zeros_like(a_ref)
    a_ref[:, :n] = c_ref[...]
    shape = a_ref.shape
    sub = lax.broadcasted_iota(jnp.int32, shape, 0)
    lane = lax.broadcasted_iota(jnp.int32, shape, 1)
    b_ref[...] = jnp.where(sub == lane, 1.0, 0.0).astype(jnp.float32)

    def step(k, carry):
        row_a = a_ref[pl.ds(k, 1), :]
        row_b = b_ref[pl.ds(k, 1), :]
        a = a_ref[...]
        pivot = jnp.sum(jnp.where(lane[:1] == k, row_a, 0.0), axis=1, keepdims=True)
        col = jnp.sum(jnp.where(lane == k, a, 0.0), axis=1, keepdims=True)
        factor = jnp.where(sub[:, :1] > k, col, 0.0) / pivot
        a_ref[...] = a - factor * row_a
        b_ref[...] = b_ref[...] - factor * row_b
        return carry

    lax.fori_loop(0, n, step, 0)
    a = a_ref[...]
    diag = jnp.sum(jnp.where(sub == lane, a, 0.0), axis=1, keepdims=True)
    o_ref[...] = (b_ref[...] / jnp.sqrt(diag))[:, :n]


def lower_inverse(c):
    n = c.shape[0]
    wide = ((n + 127) // 128) * 128
    return pl.pallas_call(
        inverse_kernel,
        out_shape=jax.ShapeDtypeStruct((n, n), jnp.float32),
        in_specs=[vspec()],
        out_specs=vspec(),
        scratch_shapes=[pltpu.VMEM((n, wide), jnp.float32), pltpu.VMEM((n, wide), jnp.float32)],
    )(c)


def vspec():
    return pl.BlockSpec(memory_space=pltpu.VMEM)


def grams(rows, f, h):
    nb = f.shape[0] // rows
    out = jax.ShapeDtypeStruct((nb, nb), jnp.float32)
    return pl.pallas_call(
        lambda *refs: gram_kernel(rows, *refs),
        out_shape=(out, out),
        in_specs=[vspec(), vspec()],
        out_specs=(vspec(), vspec()),
    )(f, h)


def rotate(rows, m, f):
    return pl.pallas_call(
        lambda *refs: rotate_kernel(rows, *refs),
        out_shape=jax.ShapeDtypeStruct(f.shape, jnp.float32),
        in_specs=[vspec(), vspec()],
        out_specs=vspec(),
    )(m, f)


def local(psi, potential):
    bdev = psi.shape[0]
    depth, rows_y, rows_x = (psi.shape[1], psi.shape[2], psi.shape[3])
    nbands = bdev * lax.axis_size("band")
    ncells = depth * lax.axis_size("dom") * rows_y * rows_x
    own_start = lax.axis_index("band") * bdev

    def apply(field):
        padded = extended(field, (("dom", 1),), stencil_reach)
        return hamiltonian(field, padded, potential)

    chunks = CHUNKS if bdev % CHUNKS == 0 else 1
    width = bdev // chunks
    previous = [psi[i * width : (i + 1) * width] for i in range(chunks)]
    current = [(apply(p) - center * p) / half for p in previous]
    for order in range(1, DEGREE):
        following = [2.0 / half * (apply(c) - center * c) - p for c, p in zip(current, previous)]
        previous, current = (current, following)
    image = jnp.concatenate([apply(c) for c in current])
    current = jnp.concatenate(current)
    groups = lax.axis_size("band")
    rows = depth * rows_y * rows_x // groups // rows_x
    lanes = rows_x
    chunked = jnp.stack([current, image]).reshape(2, bdev, groups, rows, lanes)
    spread = lax.all_to_all(chunked, "band", 2, 2, tiled=True)
    flat_cd = spread[0].reshape(bdev * groups * rows, lanes)
    image_cd = spread[1].reshape(bdev * groups * rows, lanes)
    c_perm, g_perm = grams(rows, flat_cd, image_cd)
    below = lax.broadcasted_iota(jnp.int32, (nbands, nbands), 0) >= lax.broadcasted_iota(
        jnp.int32, (nbands, nbands), 1
    )
    packed = jnp.concatenate(
        [jnp.where(below, c_perm, g_perm), jnp.diagonal(g_perm)[None], jnp.zeros((7, nbands), jnp.float32)]
    )
    packed = mesh_sum(packed) / ncells
    tri, g_diag = packed[:nbands], packed[nbands]
    c_sum = jnp.where(below, tri, tri.T)
    g_sum = jnp.where(below, tri.T, tri)
    g_sum = jnp.where(jnp.eye(nbands, dtype=bool), g_diag[None, :], g_sum)

    def to_true(m):
        return m.reshape(bdev, groups, bdev, groups).transpose(1, 0, 3, 2).reshape(nbands, nbands)

    def to_perm(m):
        return m.reshape(groups, bdev, groups, bdev).transpose(1, 0, 3, 2).reshape(nbands, nbands)

    correlation, gram = to_true(c_sum), to_true(g_sum)
    inverse = lower_inverse(correlation)
    basis_cd = rotate(rows, to_perm(inverse), flat_cd).reshape(bdev, groups, rows, lanes)
    basis = lax.all_to_all(basis_cd, "band", 1, 1, tiled=True).reshape(psi.shape)
    own_rows = lax.dynamic_slice_in_dim(inverse, own_start, bdev, 0)
    projected = hp_dot(hp_dot(own_rows, gram, ((1,), (0,))), inverse, ((1,), (1,)))
    return (basis, projected)


def solution(mesh):
    in_specs = (P("band", "dom", None, None), P("dom", None, None))
    out_specs = (P("band", "dom", None, None), P("band", None))
    return jax.shard_map(local, mesh=mesh, in_specs=in_specs, out_specs=out_specs, check_vma=False)
```

```python
import jax
import jax.numpy as jnp
from jax import lax
from jax.experimental import pallas as pl
from jax.experimental.pallas import tpu as pltpu
from jax.sharding import PartitionSpec as P

DEGREE = 4
CHUNKS = 2


stencil_coef = (-205.0 / 72.0, 8.0 / 5.0, -1.0 / 5.0, 8.0 / 315.0, -1.0 / 560.0)
stencil_reach = 4
center = 5.25
half = 4.75


def extended(array, sides, width):
    for axis, dim in sides:
        count, length = (lax.axis_size(axis), array.shape[dim])
        up = [(i, (i + 1) % count) for i in range(count)]
        down = [(j, i) for i, j in up]
        last = lax.slice_in_dim(array, length - width, length, axis=dim)
        initial = lax.slice_in_dim(array, 0, width, axis=dim)
        before = lax.ppermute(last, axis, up)
        after = lax.ppermute(initial, axis, down)
        array = jnp.concatenate([before, array, after], axis=dim)
    return array


def hp_dot(left, right, dims):
    return lax.dot_general(
        left,
        right,
        (dims, ((), ())),
        precision=lax.Precision.HIGHEST,
        preferred_element_type=jnp.float32,
    )


def hamiltonian(field, padded, potential):
    depth = field.shape[1]
    laplace = 3.0 * stencil_coef[0] * field
    for reach in range(1, 5):
        near = (
            padded[:, stencil_reach + reach : stencil_reach + reach + depth]
            + padded[:, stencil_reach - reach : stencil_reach - reach + depth]
        )
        near = near + jnp.roll(field, reach, 2) + jnp.roll(field, -reach, 2)
        near = near + jnp.roll(field, reach, 3) + jnp.roll(field, -reach, 3)
        laplace = laplace + stencil_coef[reach] * near
    return potential[None] * field - 0.5 * laplace


def group_sum(x, axis, stride, size):
    count = lax.axis_size(axis)
    pos = (lax.axis_index(axis) // stride) % size
    received = [x]
    for shift in range(1, size):
        pairs = []
        for i in range(count):
            p = (i // stride) % size
            pairs.append((i, i + (((p + shift) % size) - p) * stride))
        received.append(lax.ppermute(x, axis, pairs))
    def at(p):
        value = received[0]
        for shift in range(1, size):
            value = jnp.where((pos - p) % size == shift, received[shift], value)
        return value
    values = [at(p) for p in range(size)]
    while len(values) > 1:
        values = [values[i] + values[i + 1] for i in range(0, len(values), 2)]
    return values[0]


def mesh_sum(x):
    x = group_sum(x, "dom", 1, 2)
    x = group_sum(x, "dom", 2, lax.axis_size("dom") // 2)
    x = group_sum(x, "band", 1, 4)
    return group_sum(x, "band", 4, lax.axis_size("band") // 4)


def gram_kernel(rows, f_ref, h_ref, c_ref, g_ref):
    nb = c_ref.shape[0]
    c_ref[...] = jnp.zeros_like(c_ref)
    g_ref[...] = jnp.zeros_like(g_ref)
    for r in range(rows):
        f = f_ref[pl.ds(r, nb, stride=rows), :]
        h = h_ref[pl.ds(r, nb, stride=rows), :]
        c_ref[...] += hp_dot(f, f, ((1,), (1,)))
        g_ref[...] += hp_dot(f, h, ((1,), (1,)))


def rotate_kernel(rows, m_ref, f_ref, o_ref):
    nb = m_ref.shape[0]
    for r in range(rows):
        o_ref[pl.ds(r, nb, stride=rows), :] = hp_dot(
            m_ref[...], f_ref[pl.ds(r, nb, stride=rows), :], ((1,), (0,))
        )


def inverse_kernel(c_ref, o_ref, a_ref, b_ref):
    n = c_ref.shape[0]
    a_ref[...] = jnp.zeros_like(a_ref)
    a_ref[:, :n] = c_ref[...]
    shape = a_ref.shape
    sub = lax.broadcasted_iota(jnp.int32, shape, 0)
    lane = lax.broadcasted_iota(jnp.int32, shape, 1)
    b_ref[...] = jnp.where(sub == lane, 1.0, 0.0).astype(jnp.float32)

    def step(k, carry):
        row_a = a_ref[pl.ds(k, 1), :]
        row_b = b_ref[pl.ds(k, 1), :]
        a = a_ref[...]
        pivot = jnp.sum(jnp.where(lane[:1] == k, row_a, 0.0), axis=1, keepdims=True)
        col = jnp.sum(jnp.where(lane == k, a, 0.0), axis=1, keepdims=True)
        factor = jnp.where(sub[:, :1] > k, col, 0.0) / pivot
        a_ref[...] = a - factor * row_a
        b_ref[...] = b_ref[...] - factor * row_b
        return carry

    lax.fori_loop(0, n, step, 0)
    a = a_ref[...]
    diag = jnp.sum(jnp.where(sub == lane, a, 0.0), axis=1, keepdims=True)
    o_ref[...] = (b_ref[...] / jnp.sqrt(diag))[:, :n]


def lower_inverse(c):
    n = c.shape[0]
    wide = ((n + 127) // 128) * 128
    return pl.pallas_call(
        inverse_kernel,
        out_shape=jax.ShapeDtypeStruct((n, n), jnp.float32),
        in_specs=[vspec()],
        out_specs=vspec(),
        scratch_shapes=[pltpu.VMEM((n, wide), jnp.float32), pltpu.VMEM((n, wide), jnp.float32)],
    )(c)


def vspec():
    return pl.BlockSpec(memory_space=pltpu.VMEM)


def grams(rows, f, h):
    nb = f.shape[0] // rows
    out = jax.ShapeDtypeStruct((nb, nb), jnp.float32)
    return pl.pallas_call(
        lambda *refs: gram_kernel(rows, *refs),
        out_shape=(out, out),
        in_specs=[vspec(), vspec()],
        out_specs=(vspec(), vspec()),
    )(f, h)


def rotate(rows, m, f):
    return pl.pallas_call(
        lambda *refs: rotate_kernel(rows, *refs),
        out_shape=jax.ShapeDtypeStruct(f.shape, jnp.float32),
        in_specs=[vspec(), vspec()],
        out_specs=vspec(),
    )(m, f)


def stencil_kernel(mode, f_ref, lo_ref, hi_ref, prev_ref, pot_ref, o_ref):
    depth = f_ref.shape[1]
    rows, lanes = f_ref.shape[2], f_ref.shape[3]

    def plane(z):
        if z < 0:
            return lo_ref[0, depth + z]
        if z >= depth:
            return hi_ref[0, z - depth]
        return f_ref[0, z]

    for z in range(depth):
        v = f_ref[0, z]
        laplace = 3.0 * stencil_coef[0] * v
        for reach in range(1, stencil_reach + 1):
            near = plane(z + reach) + plane(z - reach)
            near = near + pltpu.roll(v, reach, 0) + pltpu.roll(v, rows - reach, 0)
            near = near + pltpu.roll(v, reach, 1) + pltpu.roll(v, lanes - reach, 1)
            laplace = laplace + stencil_coef[reach] * near
        h = pot_ref[z] * v - 0.5 * laplace
        if mode == 0:
            out = (h - center * v) / half
        elif mode == 1:
            out = 2.0 / half * (h - center * v) - prev_ref[0, z]
        else:
            out = h
        o_ref[0, z] = out


def stencil(mode, f, lo, hi, prev, pot):
    band = pl.BlockSpec((1,) + f.shape[1:], lambda b: (b, 0, 0, 0))
    return pl.pallas_call(
        lambda *refs: stencil_kernel(mode, *refs),
        out_shape=jax.ShapeDtypeStruct(f.shape, jnp.float32),
        grid=(f.shape[0],),
        in_specs=[band, band, band, band, pl.BlockSpec(pot.shape, lambda b: (0, 0, 0))],
        out_specs=band,
        cost_estimate=pl.CostEstimate(
            flops=60 * f.size, transcendentals=0, bytes_accessed=4 * (5 * f.size + pot.size)
        ),
    )(f, lo, hi, prev, pot)


def local(psi, potential):
    bdev = psi.shape[0]
    depth, rows_y, rows_x = (psi.shape[1], psi.shape[2], psi.shape[3])
    nbands = bdev * lax.axis_size("band")
    ncells = depth * lax.axis_size("dom") * rows_y * rows_x
    own_start = lax.axis_index("band") * bdev

    def halo(field):
        count = lax.axis_size("dom")
        up = [(i, (i + 1) % count) for i in range(count)]
        down = [(j, i) for i, j in up]
        lo = lax.ppermute(field[:, depth - stencil_reach :], "dom", up)
        hi = lax.ppermute(field[:, :stencil_reach], "dom", down)
        return lo, hi

    def step(mode, field, prev):
        lo, hi = halo(field)
        return stencil(mode, field, lo, hi, prev, potential)

    chunks = CHUNKS if bdev % CHUNKS == 0 else 1
    width = bdev // chunks
    previous = [psi[i * width : (i + 1) * width] for i in range(chunks)]
    current = [step(0, p, p) for p in previous]
    for order in range(1, DEGREE):
        following = [step(1, c, p) for c, p in zip(current, previous)]
        previous, current = (current, following)
    image = jnp.concatenate([step(2, c, c) for c in current])
    current = jnp.concatenate(current)
    groups = lax.axis_size("band")
    rows = depth * rows_y * rows_x // groups // rows_x
    lanes = rows_x
    chunked = jnp.stack([current, image]).reshape(2, bdev, groups, rows, lanes)
    spread = lax.all_to_all(chunked, "band", 2, 2, tiled=True)
    flat_cd = spread[0].reshape(bdev * groups * rows, lanes)
    image_cd = spread[1].reshape(bdev * groups * rows, lanes)
    c_perm, g_perm = grams(rows, flat_cd, image_cd)
    below = lax.broadcasted_iota(jnp.int32, (nbands, nbands), 0) >= lax.broadcasted_iota(
        jnp.int32, (nbands, nbands), 1
    )
    packed = jnp.concatenate(
        [jnp.where(below, c_perm, g_perm), jnp.diagonal(g_perm)[None], jnp.zeros((7, nbands), jnp.float32)]
    )
    packed = mesh_sum(packed) / ncells
    tri, g_diag = packed[:nbands], packed[nbands]
    c_sum = jnp.where(below, tri, tri.T)
    g_sum = jnp.where(below, tri.T, tri)
    g_sum = jnp.where(jnp.eye(nbands, dtype=bool), g_diag[None, :], g_sum)

    def to_true(m):
        return m.reshape(bdev, groups, bdev, groups).transpose(1, 0, 3, 2).reshape(nbands, nbands)

    def to_perm(m):
        return m.reshape(groups, bdev, groups, bdev).transpose(1, 0, 3, 2).reshape(nbands, nbands)

    correlation, gram = to_true(c_sum), to_true(g_sum)
    inverse = lower_inverse(correlation)
    basis_cd = rotate(rows, to_perm(inverse), flat_cd).reshape(bdev, groups, rows, lanes)
    basis = lax.all_to_all(basis_cd, "band", 1, 1, tiled=True).reshape(psi.shape)
    own_rows = lax.dynamic_slice_in_dim(inverse, own_start, bdev, 0)
    projected = hp_dot(hp_dot(own_rows, gram, ((1,), (0,))), inverse, ((1,), (1,)))
    return (basis, projected)


def solution(mesh):
    in_specs = (P("band", "dom", None, None), P("dom", None, None))
    out_specs = (P("band", "dom", None, None), P("band", None))
    return jax.shard_map(local, mesh=mesh, in_specs=in_specs, out_specs=out_specs, check_vma=False)
```

```python
import jax
import jax.numpy as jnp
from jax import lax
from jax.experimental import pallas as pl
from jax.experimental.pallas import tpu as pltpu
from jax.sharding import PartitionSpec as P

DEGREE = 4
CHUNKS = 2


stencil_coef = (-205.0 / 72.0, 8.0 / 5.0, -1.0 / 5.0, 8.0 / 315.0, -1.0 / 560.0)
stencil_reach = 4
center = 5.25
half = 4.75


def extended(array, sides, width):
    for axis, dim in sides:
        count, length = (lax.axis_size(axis), array.shape[dim])
        up = [(i, (i + 1) % count) for i in range(count)]
        down = [(j, i) for i, j in up]
        last = lax.slice_in_dim(array, length - width, length, axis=dim)
        initial = lax.slice_in_dim(array, 0, width, axis=dim)
        before = lax.ppermute(last, axis, up)
        after = lax.ppermute(initial, axis, down)
        array = jnp.concatenate([before, array, after], axis=dim)
    return array


def hp_dot(left, right, dims):
    return lax.dot_general(
        left,
        right,
        (dims, ((), ())),
        precision=lax.Precision.HIGHEST,
        preferred_element_type=jnp.float32,
    )


def hamiltonian(field, padded, potential):
    depth = field.shape[1]
    laplace = 3.0 * stencil_coef[0] * field
    for reach in range(1, 5):
        near = (
            padded[:, stencil_reach + reach : stencil_reach + reach + depth]
            + padded[:, stencil_reach - reach : stencil_reach - reach + depth]
        )
        near = near + jnp.roll(field, reach, 2) + jnp.roll(field, -reach, 2)
        near = near + jnp.roll(field, reach, 3) + jnp.roll(field, -reach, 3)
        laplace = laplace + stencil_coef[reach] * near
    return potential[None] * field - 0.5 * laplace


def group_sum(x, axis, stride, size):
    count = lax.axis_size(axis)
    pos = (lax.axis_index(axis) // stride) % size
    received = [x]
    for shift in range(1, size):
        pairs = []
        for i in range(count):
            p = (i // stride) % size
            pairs.append((i, i + (((p + shift) % size) - p) * stride))
        received.append(lax.ppermute(x, axis, pairs))
    def at(p):
        value = received[0]
        for shift in range(1, size):
            value = jnp.where((pos - p) % size == shift, received[shift], value)
        return value
    values = [at(p) for p in range(size)]
    while len(values) > 1:
        values = [values[i] + values[i + 1] for i in range(0, len(values), 2)]
    return values[0]


def mesh_sum(x):
    x = group_sum(x, "dom", 1, 2)
    x = group_sum(x, "dom", 2, lax.axis_size("dom") // 2)
    x = group_sum(x, "band", 1, 4)
    return group_sum(x, "band", 4, lax.axis_size("band") // 4)


def gram_kernel(rows, f_ref, h_ref, c_ref, g_ref):
    nb = c_ref.shape[0]
    c_ref[...] = jnp.zeros_like(c_ref)
    g_ref[...] = jnp.zeros_like(g_ref)
    for r in range(rows):
        f = f_ref[pl.ds(r, nb, stride=rows), :]
        h = h_ref[pl.ds(r, nb, stride=rows), :]
        c_ref[...] += hp_dot(f, f, ((1,), (1,)))
        g_ref[...] += hp_dot(f, h, ((1,), (1,)))


def rotate_kernel(rows, m_ref, f_ref, o_ref):
    nb = m_ref.shape[0]
    for r in range(rows):
        o_ref[pl.ds(r, nb, stride=rows), :] = hp_dot(
            m_ref[...], f_ref[pl.ds(r, nb, stride=rows), :], ((1,), (0,))
        )


def inverse_kernel(c_ref, o_ref, a_ref, b_ref):
    n = c_ref.shape[0]
    a_ref[...] = jnp.zeros_like(a_ref)
    a_ref[:, :n] = c_ref[...]
    shape = a_ref.shape
    sub = lax.broadcasted_iota(jnp.int32, shape, 0)
    lane = lax.broadcasted_iota(jnp.int32, shape, 1)
    b_ref[...] = jnp.where(sub == lane, 1.0, 0.0).astype(jnp.float32)
    tile = 128
    tiles = shape[1] // tile

    def segment(k0, k1, r0):
        ta, tb = k0 // tile, (k1 - 1) // tile + 1
        rows = shape[0] - r0

        def step(k, carry):
            row_a = a_ref[pl.ds(k, 1), :][:, ta * tile :]
            row_b = b_ref[pl.ds(k, 1), :][:, : tb * tile]
            a = a_ref[r0:, ta * tile :]
            lane_a = lax.broadcasted_iota(jnp.int32, a.shape, 1) + ta * tile
            pivot = jnp.sum(jnp.where(lane_a[:1] == k, row_a, 0.0), axis=1, keepdims=True)
            col = jnp.sum(jnp.where(lane_a == k, a, 0.0), axis=1, keepdims=True)
            below = lax.broadcasted_iota(jnp.int32, (rows, 1), 0) + r0 > k
            factor = jnp.where(below, col, 0.0) / pivot
            a_ref[r0:, ta * tile :] = a - factor * row_a
            b_ref[r0:, : tb * tile] = b_ref[r0:, : tb * tile] - factor * row_b
            return carry

        lax.fori_loop(k0, k1, step, 0)

    bounds = sorted({0, n} | {t * tile for t in range(1, tiles) if t * tile < n})
    for k0, k1 in zip(bounds[:-1], bounds[1:]):
        segment(k0, k1, (k0 // 8) * 8)
    a = a_ref[...]
    diag = jnp.sum(jnp.where(sub == lane, a, 0.0), axis=1, keepdims=True)
    o_ref[...] = (b_ref[...] / jnp.sqrt(diag))[:, :n]


def lower_inverse(c):
    n = c.shape[0]
    wide = ((n + 127) // 128) * 128
    return pl.pallas_call(
        inverse_kernel,
        out_shape=jax.ShapeDtypeStruct((n, n), jnp.float32),
        in_specs=[vspec()],
        out_specs=vspec(),
        scratch_shapes=[pltpu.VMEM((n, wide), jnp.float32), pltpu.VMEM((n, wide), jnp.float32)],
    )(c)


def vspec():
    return pl.BlockSpec(memory_space=pltpu.VMEM)


def grams(rows, f, h):
    nb = f.shape[0] // rows
    out = jax.ShapeDtypeStruct((nb, nb), jnp.float32)
    return pl.pallas_call(
        lambda *refs: gram_kernel(rows, *refs),
        out_shape=(out, out),
        in_specs=[vspec(), vspec()],
        out_specs=(vspec(), vspec()),
    )(f, h)


def rotate(rows, m, f):
    return pl.pallas_call(
        lambda *refs: rotate_kernel(rows, *refs),
        out_shape=jax.ShapeDtypeStruct(f.shape, jnp.float32),
        in_specs=[vspec(), vspec()],
        out_specs=vspec(),
    )(m, f)


def local(psi, potential):
    bdev = psi.shape[0]
    depth, rows_y, rows_x = (psi.shape[1], psi.shape[2], psi.shape[3])
    nbands = bdev * lax.axis_size("band")
    ncells = depth * lax.axis_size("dom") * rows_y * rows_x
    own_start = lax.axis_index("band") * bdev

    def apply(field):
        padded = extended(field, (("dom", 1),), stencil_reach)
        return hamiltonian(field, padded, potential)

    chunks = CHUNKS if bdev % CHUNKS == 0 else 1
    width = bdev // chunks
    previous = [psi[i * width : (i + 1) * width] for i in range(chunks)]
    current = [(apply(p) - center * p) / half for p in previous]
    for order in range(1, DEGREE):
        following = [2.0 / half * (apply(c) - center * c) - p for c, p in zip(current, previous)]
        previous, current = (current, following)
    image = jnp.concatenate([apply(c) for c in current])
    current = jnp.concatenate(current)
    groups = lax.axis_size("band")
    rows = depth * rows_y * rows_x // groups // rows_x
    lanes = rows_x
    chunked = jnp.stack([current, image]).reshape(2, bdev, groups, rows, lanes)
    spread = lax.all_to_all(chunked, "band", 2, 2, tiled=True)
    flat_cd = spread[0].reshape(bdev * groups * rows, lanes)
    image_cd = spread[1].reshape(bdev * groups * rows, lanes)
    c_perm, g_perm = grams(rows, flat_cd, image_cd)
    below = lax.broadcasted_iota(jnp.int32, (nbands, nbands), 0) >= lax.broadcasted_iota(
        jnp.int32, (nbands, nbands), 1
    )
    packed = jnp.concatenate(
        [jnp.where(below, c_perm, g_perm), jnp.diagonal(g_perm)[None], jnp.zeros((7, nbands), jnp.float32)]
    )
    packed = mesh_sum(packed) / ncells
    tri, g_diag = packed[:nbands], packed[nbands]
    c_sum = jnp.where(below, tri, tri.T)
    g_sum = jnp.where(below, tri.T, tri)
    g_sum = jnp.where(jnp.eye(nbands, dtype=bool), g_diag[None, :], g_sum)

    def to_true(m):
        return m.reshape(bdev, groups, bdev, groups).transpose(1, 0, 3, 2).reshape(nbands, nbands)

    def to_perm(m):
        return m.reshape(groups, bdev, groups, bdev).transpose(1, 0, 3, 2).reshape(nbands, nbands)

    correlation, gram = to_true(c_sum), to_true(g_sum)
    inverse = lower_inverse(correlation)
    basis_cd = rotate(rows, to_perm(inverse), flat_cd).reshape(bdev, groups, rows, lanes)
    basis = lax.all_to_all(basis_cd, "band", 1, 1, tiled=True).reshape(psi.shape)
    own_rows = lax.dynamic_slice_in_dim(inverse, own_start, bdev, 0)
    projected = hp_dot(hp_dot(own_rows, gram, ((1,), (0,))), inverse, ((1,), (1,)))
    return (basis, projected)


def solution(mesh):
    in_specs = (P("band", "dom", None, None), P("dom", None, None))
    out_specs = (P("band", "dom", None, None), P("band", None))
    return jax.shard_map(local, mesh=mesh, in_specs=in_specs, out_specs=out_specs, check_vma=False)
```

```python
import jax
import jax.numpy as jnp
from jax import lax
from jax.experimental import pallas as pl
from jax.experimental.pallas import tpu as pltpu
from jax.sharding import PartitionSpec as P

DEGREE = 4
CHUNKS = 2


stencil_coef = (-205.0 / 72.0, 8.0 / 5.0, -1.0 / 5.0, 8.0 / 315.0, -1.0 / 560.0)
stencil_reach = 4
center = 5.25
half = 4.75


def extended(array, sides, width):
    for axis, dim in sides:
        count, length = (lax.axis_size(axis), array.shape[dim])
        up = [(i, (i + 1) % count) for i in range(count)]
        down = [(j, i) for i, j in up]
        last = lax.slice_in_dim(array, length - width, length, axis=dim)
        initial = lax.slice_in_dim(array, 0, width, axis=dim)
        before = lax.ppermute(last, axis, up)
        after = lax.ppermute(initial, axis, down)
        array = jnp.concatenate([before, array, after], axis=dim)
    return array


def hp_dot(left, right, dims):
    return lax.dot_general(
        left,
        right,
        (dims, ((), ())),
        precision=lax.Precision.HIGHEST,
        preferred_element_type=jnp.float32,
    )


def hamiltonian(field, padded, potential):
    depth = field.shape[1]
    laplace = 3.0 * stencil_coef[0] * field
    for reach in range(1, 5):
        near = (
            padded[:, stencil_reach + reach : stencil_reach + reach + depth]
            + padded[:, stencil_reach - reach : stencil_reach - reach + depth]
        )
        near = near + jnp.roll(field, reach, 2) + jnp.roll(field, -reach, 2)
        near = near + jnp.roll(field, reach, 3) + jnp.roll(field, -reach, 3)
        laplace = laplace + stencil_coef[reach] * near
    return potential[None] * field - 0.5 * laplace


def group_sum(x, axis, stride, size):
    count = lax.axis_size(axis)
    pos = (lax.axis_index(axis) // stride) % size
    received = [x]
    for shift in range(1, size):
        pairs = []
        for i in range(count):
            p = (i // stride) % size
            pairs.append((i, i + (((p + shift) % size) - p) * stride))
        received.append(lax.ppermute(x, axis, pairs))
    def at(p):
        value = received[0]
        for shift in range(1, size):
            value = jnp.where((pos - p) % size == shift, received[shift], value)
        return value
    values = [at(p) for p in range(size)]
    while len(values) > 1:
        values = [values[i] + values[i + 1] for i in range(0, len(values), 2)]
    return values[0]


def mesh_sum(x):
    x = group_sum(x, "dom", 1, 2)
    x = group_sum(x, "dom", 2, lax.axis_size("dom") // 2)
    x = group_sum(x, "band", 1, 4)
    return group_sum(x, "band", 4, lax.axis_size("band") // 4)


def gram_kernel(rows, f_ref, h_ref, c_ref, g_ref):
    nb = c_ref.shape[0]
    c_ref[...] = jnp.zeros_like(c_ref)
    g_ref[...] = jnp.zeros_like(g_ref)
    for r in range(rows):
        f = f_ref[pl.ds(r, nb, stride=rows), :]
        h = h_ref[pl.ds(r, nb, stride=rows), :]
        c_ref[...] += hp_dot(f, f, ((1,), (1,)))
        g_ref[...] += hp_dot(f, h, ((1,), (1,)))


def rotate_kernel(rows, m_ref, f_ref, o_ref):
    nb = m_ref.shape[0]
    for r in range(rows):
        o_ref[pl.ds(r, nb, stride=rows), :] = hp_dot(
            m_ref[...], f_ref[pl.ds(r, nb, stride=rows), :], ((1,), (0,))
        )


def inverse_kernel(c_ref, o_ref, a_ref, b_ref):
    n = c_ref.shape[0]
    a_ref[...] = jnp.zeros_like(a_ref)
    a_ref[:, :n] = c_ref[...]
    shape = a_ref.shape
    sub = lax.broadcasted_iota(jnp.int32, shape, 0)
    lane = lax.broadcasted_iota(jnp.int32, shape, 1)
    b_ref[...] = jnp.where(sub == lane, 1.0, 0.0).astype(jnp.float32)
    tile = 128
    tiles = shape[1] // tile

    def segment(k0, k1, r0):
        ta, tb = k0 // tile, (k1 - 1) // tile + 1
        rows = shape[0] - r0

        def step(k, carry):
            row_a = a_ref[pl.ds(k, 1), :][:, ta * tile :]
            row_b = b_ref[pl.ds(k, 1), :][:, : tb * tile]
            a = a_ref[r0:, ta * tile :]
            lane_a = lax.broadcasted_iota(jnp.int32, a.shape, 1) + ta * tile
            pivot = jnp.sum(jnp.where(lane_a[:1] == k, row_a, 0.0), axis=1, keepdims=True)
            col = jnp.sum(jnp.where(lane_a == k, a, 0.0), axis=1, keepdims=True)
            below = lax.broadcasted_iota(jnp.int32, (rows, 1), 0) + r0 > k
            factor = jnp.where(below, col, 0.0) / pivot
            a_ref[r0:, ta * tile :] = a - factor * row_a
            b_ref[r0:, : tb * tile] = b_ref[r0:, : tb * tile] - factor * row_b
            return carry

        lax.fori_loop(k0, k1, step, 0)

    bounds = sorted({0, n} | {t * tile for t in range(1, tiles) if t * tile < n})
    for k0, k1 in zip(bounds[:-1], bounds[1:]):
        segment(k0, k1, (k0 // 8) * 8)
    a = a_ref[...]
    diag = jnp.sum(jnp.where(sub == lane, a, 0.0), axis=1, keepdims=True)
    o_ref[...] = (b_ref[...] / jnp.sqrt(diag))[:, :n]


def lower_inverse(c):
    n = c.shape[0]
    wide = ((n + 127) // 128) * 128
    return pl.pallas_call(
        inverse_kernel,
        out_shape=jax.ShapeDtypeStruct((n, n), jnp.float32),
        in_specs=[vspec()],
        out_specs=vspec(),
        scratch_shapes=[pltpu.VMEM((n, wide), jnp.float32), pltpu.VMEM((n, wide), jnp.float32)],
    )(c)


def vspec():
    return pl.BlockSpec(memory_space=pltpu.VMEM)


def grams(rows, f, h):
    nb = f.shape[0] // rows
    out = jax.ShapeDtypeStruct((nb, nb), jnp.float32)
    return pl.pallas_call(
        lambda *refs: gram_kernel(rows, *refs),
        out_shape=(out, out),
        in_specs=[vspec(), vspec()],
        out_specs=(vspec(), vspec()),
    )(f, h)


def rotate(rows, m, f):
    return pl.pallas_call(
        lambda *refs: rotate_kernel(rows, *refs),
        out_shape=jax.ShapeDtypeStruct(f.shape, jnp.float32),
        in_specs=[vspec(), vspec()],
        out_specs=vspec(),
    )(m, f)


def local(psi, potential):
    bdev = psi.shape[0]
    depth, rows_y, rows_x = (psi.shape[1], psi.shape[2], psi.shape[3])
    nbands = bdev * lax.axis_size("band")
    ncells = depth * lax.axis_size("dom") * rows_y * rows_x
    own_start = lax.axis_index("band") * bdev

    def apply(field):
        padded = extended(field, (("dom", 1),), stencil_reach)
        return hamiltonian(field, padded, potential)

    chunks = CHUNKS if bdev % CHUNKS == 0 else 1
    width = bdev // chunks
    previous = [psi[i * width : (i + 1) * width] for i in range(chunks)]
    current = [(apply(p) - center * p) / half for p in previous]
    for order in range(1, DEGREE):
        following = [2.0 / half * (apply(c) - center * c) - p for c, p in zip(current, previous)]
        previous, current = (current, following)
    filtered = jnp.concatenate(current)
    image = jnp.concatenate([apply(c) for c in current])
    current = filtered
    groups = lax.axis_size("band")
    rows = depth * rows_y * rows_x // groups // rows_x
    lanes = rows_x
    def spread(x):
        y = lax.all_to_all(x.reshape(bdev, groups, rows, lanes), "band", 1, 1, tiled=True)
        return y.reshape(bdev * groups * rows, lanes)

    flat_cd = spread(current)
    image_cd = spread(image)
    c_perm, g_perm = grams(rows, flat_cd, image_cd)
    below = lax.broadcasted_iota(jnp.int32, (nbands, nbands), 0) >= lax.broadcasted_iota(
        jnp.int32, (nbands, nbands), 1
    )
    packed = jnp.concatenate(
        [jnp.where(below, c_perm, g_perm), jnp.diagonal(g_perm)[None], jnp.zeros((7, nbands), jnp.float32)]
    )
    packed = mesh_sum(packed) / ncells
    tri, g_diag = packed[:nbands], packed[nbands]
    c_sum = jnp.where(below, tri, tri.T)
    g_sum = jnp.where(below, tri.T, tri)
    g_sum = jnp.where(jnp.eye(nbands, dtype=bool), g_diag[None, :], g_sum)

    def to_true(m):
        return m.reshape(bdev, groups, bdev, groups).transpose(1, 0, 3, 2).reshape(nbands, nbands)

    def to_perm(m):
        return m.reshape(groups, bdev, groups, bdev).transpose(1, 0, 3, 2).reshape(nbands, nbands)

    correlation, gram = to_true(c_sum), to_true(g_sum)
    inverse = lower_inverse(correlation)
    basis_cd = rotate(rows, to_perm(inverse), flat_cd).reshape(bdev, groups, rows, lanes)
    basis = lax.all_to_all(basis_cd, "band", 1, 1, tiled=True).reshape(psi.shape)
    own_rows = lax.dynamic_slice_in_dim(inverse, own_start, bdev, 0)
    projected = hp_dot(hp_dot(own_rows, gram, ((1,), (0,))), inverse, ((1,), (1,)))
    return (basis, projected)


def solution(mesh):
    in_specs = (P("band", "dom", None, None), P("dom", None, None))
    out_specs = (P("band", "dom", None, None), P("band", None))
    return jax.shard_map(local, mesh=mesh, in_specs=in_specs, out_specs=out_specs, check_vma=False)
```

```python
import jax
import jax.numpy as jnp
from jax import lax
from jax.experimental import pallas as pl
from jax.experimental.pallas import tpu as pltpu
from jax.sharding import PartitionSpec as P

DEGREE = 4
CHUNKS = 2


stencil_coef = (-205.0 / 72.0, 8.0 / 5.0, -1.0 / 5.0, 8.0 / 315.0, -1.0 / 560.0)
stencil_reach = 4
center = 5.25
half = 4.75


def extended(array, sides, width):
    for axis, dim in sides:
        count, length = (lax.axis_size(axis), array.shape[dim])
        up = [(i, (i + 1) % count) for i in range(count)]
        down = [(j, i) for i, j in up]
        last = lax.slice_in_dim(array, length - width, length, axis=dim)
        initial = lax.slice_in_dim(array, 0, width, axis=dim)
        before = lax.ppermute(last, axis, up)
        after = lax.ppermute(initial, axis, down)
        array = jnp.concatenate([before, array, after], axis=dim)
    return array


def hp_dot(left, right, dims):
    return lax.dot_general(
        left,
        right,
        (dims, ((), ())),
        precision=lax.Precision.HIGHEST,
        preferred_element_type=jnp.float32,
    )


def hamiltonian(field, padded, potential):
    depth = field.shape[1]
    laplace = 3.0 * stencil_coef[0] * field
    for reach in range(1, 5):
        near = (
            padded[:, stencil_reach + reach : stencil_reach + reach + depth]
            + padded[:, stencil_reach - reach : stencil_reach - reach + depth]
        )
        near = near + jnp.roll(field, reach, 2) + jnp.roll(field, -reach, 2)
        near = near + jnp.roll(field, reach, 3) + jnp.roll(field, -reach, 3)
        laplace = laplace + stencil_coef[reach] * near
    return potential[None] * field - 0.5 * laplace


def group_sum(x, axis, stride, size):
    count = lax.axis_size(axis)
    pos = (lax.axis_index(axis) // stride) % size
    received = [x]
    for shift in range(1, size):
        pairs = []
        for i in range(count):
            p = (i // stride) % size
            pairs.append((i, i + (((p + shift) % size) - p) * stride))
        received.append(lax.ppermute(x, axis, pairs))
    def at(p):
        value = received[0]
        for shift in range(1, size):
            value = jnp.where((pos - p) % size == shift, received[shift], value)
        return value
    values = [at(p) for p in range(size)]
    while len(values) > 1:
        values = [values[i] + values[i + 1] for i in range(0, len(values), 2)]
    return values[0]


def mesh_sum(x):
    x = group_sum(x, "dom", 1, 2)
    x = group_sum(x, "dom", 2, lax.axis_size("dom") // 2)
    x = group_sum(x, "band", 1, 4)
    return group_sum(x, "band", 4, lax.axis_size("band") // 4)


def gram_kernel(rows, f_ref, h_ref, c_ref, g_ref):
    nb = c_ref.shape[0]
    c_ref[...] = jnp.zeros_like(c_ref)
    g_ref[...] = jnp.zeros_like(g_ref)
    for r in range(rows):
        f = f_ref[pl.ds(r, nb, stride=rows), :]
        h = h_ref[pl.ds(r, nb, stride=rows), :]
        c_ref[...] += hp_dot(f, f, ((1,), (1,)))
        g_ref[...] += hp_dot(f, h, ((1,), (1,)))


def rotate_kernel(rows, m_ref, f_ref, o_ref):
    nb = m_ref.shape[0]
    for r in range(rows):
        o_ref[pl.ds(r, nb, stride=rows), :] = hp_dot(
            m_ref[...], f_ref[pl.ds(r, nb, stride=rows), :], ((1,), (0,))
        )


def inverse_kernel(c_ref, o_ref, a_ref, b_ref):
    n = c_ref.shape[0]
    a_ref[...] = jnp.zeros_like(a_ref)
    a_ref[:, :n] = c_ref[...]
    shape = a_ref.shape
    sub = lax.broadcasted_iota(jnp.int32, shape, 0)
    lane = lax.broadcasted_iota(jnp.int32, shape, 1)
    b_ref[...] = jnp.where(sub == lane, 1.0, 0.0).astype(jnp.float32)
    tile = 128
    tiles = shape[1] // tile

    def segment(k0, k1, r0):
        ta, tb = k0 // tile, (k1 - 1) // tile + 1
        rows = shape[0] - r0

        def step(k, carry):
            row_a = a_ref[pl.ds(k, 1), :][:, ta * tile :]
            row_b = b_ref[pl.ds(k, 1), :][:, : tb * tile]
            a = a_ref[r0:, ta * tile :]
            lane_a = lax.broadcasted_iota(jnp.int32, a.shape, 1) + ta * tile
            pivot = jnp.sum(jnp.where(lane_a[:1] == k, row_a, 0.0), axis=1, keepdims=True)
            col = jnp.sum(jnp.where(lane_a == k, a, 0.0), axis=1, keepdims=True)
            below = lax.broadcasted_iota(jnp.int32, (rows, 1), 0) + r0 > k
            factor = jnp.where(below, col, 0.0) * (1.0 / pivot)
            a_ref[r0:, ta * tile :] = a - factor * row_a
            b_ref[r0:, : tb * tile] = b_ref[r0:, : tb * tile] - factor * row_b
            return carry

        lax.fori_loop(k0, k1, step, 0)

    bounds = sorted({0, n} | {t * tile for t in range(1, tiles) if t * tile < n})
    for k0, k1 in zip(bounds[:-1], bounds[1:]):
        segment(k0, k1, (k0 // 8) * 8)
    a = a_ref[...]
    diag = jnp.sum(jnp.where(sub == lane, a, 0.0), axis=1, keepdims=True)
    o_ref[...] = (b_ref[...] / jnp.sqrt(diag))[:, :n]


def lower_inverse(c):
    n = c.shape[0]
    wide = ((n + 127) // 128) * 128
    return pl.pallas_call(
        inverse_kernel,
        out_shape=jax.ShapeDtypeStruct((n, n), jnp.float32),
        in_specs=[vspec()],
        out_specs=vspec(),
        scratch_shapes=[pltpu.VMEM((n, wide), jnp.float32), pltpu.VMEM((n, wide), jnp.float32)],
    )(c)


def vspec():
    return pl.BlockSpec(memory_space=pltpu.VMEM)


def grams(rows, f, h):
    nb = f.shape[0] // rows
    out = jax.ShapeDtypeStruct((nb, nb), jnp.float32)
    return pl.pallas_call(
        lambda *refs: gram_kernel(rows, *refs),
        out_shape=(out, out),
        in_specs=[vspec(), vspec()],
        out_specs=(vspec(), vspec()),
    )(f, h)


def rotate(rows, m, f):
    return pl.pallas_call(
        lambda *refs: rotate_kernel(rows, *refs),
        out_shape=jax.ShapeDtypeStruct(f.shape, jnp.float32),
        in_specs=[vspec(), vspec()],
        out_specs=vspec(),
    )(m, f)


def local(psi, potential):
    bdev = psi.shape[0]
    depth, rows_y, rows_x = (psi.shape[1], psi.shape[2], psi.shape[3])
    nbands = bdev * lax.axis_size("band")
    ncells = depth * lax.axis_size("dom") * rows_y * rows_x
    own_start = lax.axis_index("band") * bdev

    def apply(field):
        padded = extended(field, (("dom", 1),), stencil_reach)
        return hamiltonian(field, padded, potential)

    chunks = CHUNKS if bdev % CHUNKS == 0 else 1
    width = bdev // chunks
    previous = [psi[i * width : (i + 1) * width] for i in range(chunks)]
    current = [(apply(p) - center * p) / half for p in previous]
    for order in range(1, DEGREE):
        following = [2.0 / half * (apply(c) - center * c) - p for c, p in zip(current, previous)]
        previous, current = (current, following)
    image = jnp.concatenate([apply(c) for c in current])
    current = jnp.concatenate(current)
    groups = lax.axis_size("band")
    rows = depth * rows_y * rows_x // groups // rows_x
    lanes = rows_x
    chunked = jnp.stack([current, image]).reshape(2, bdev, groups, rows, lanes)
    spread = lax.all_to_all(chunked, "band", 2, 2, tiled=True)
    flat_cd = spread[0].reshape(bdev * groups * rows, lanes)
    image_cd = spread[1].reshape(bdev * groups * rows, lanes)
    c_perm, g_perm = grams(rows, flat_cd, image_cd)
    below = lax.broadcasted_iota(jnp.int32, (nbands, nbands), 0) >= lax.broadcasted_iota(
        jnp.int32, (nbands, nbands), 1
    )
    packed = jnp.concatenate(
        [jnp.where(below, c_perm, g_perm), jnp.sum(jnp.where(lax.broadcasted_iota(jnp.int32, (nbands, nbands), 0) == lax.broadcasted_iota(jnp.int32, (nbands, nbands), 1), g_perm, 0.0), axis=0, keepdims=True), jnp.zeros((7, nbands), jnp.float32)]
    )
    packed = mesh_sum(packed) / ncells
    tri, g_diag = packed[:nbands], packed[nbands]
    c_sum = jnp.where(below, tri, tri.T)
    g_sum = jnp.where(below, tri.T, tri)
    g_sum = jnp.where(jnp.eye(nbands, dtype=bool), g_diag[None, :], g_sum)

    def to_true(m):
        return m.reshape(bdev, groups, bdev, groups).transpose(1, 0, 3, 2).reshape(nbands, nbands)

    def to_perm(m):
        return m.reshape(groups, bdev, groups, bdev).transpose(1, 0, 3, 2).reshape(nbands, nbands)

    correlation, gram = to_true(c_sum), to_true(g_sum)
    inverse = lower_inverse(correlation)
    basis_cd = rotate(rows, to_perm(inverse), flat_cd).reshape(bdev, groups, rows, lanes)
    basis = lax.all_to_all(basis_cd, "band", 1, 1, tiled=True).reshape(psi.shape)
    own_rows = lax.dynamic_slice_in_dim(inverse, own_start, bdev, 0)
    projected = hp_dot(hp_dot(own_rows, gram, ((1,), (0,))), inverse, ((1,), (1,)))
    return (basis, projected)


def solution(mesh):
    in_specs = (P("band", "dom", None, None), P("dom", None, None))
    out_specs = (P("band", "dom", None, None), P("band", None))
    return jax.shard_map(local, mesh=mesh, in_specs=in_specs, out_specs=out_specs, check_vma=False)
```

```python
import jax
import jax.numpy as jnp
from jax import lax
from jax.experimental import pallas as pl
from jax.experimental.pallas import tpu as pltpu
from jax.sharding import PartitionSpec as P

DEGREE = 4
CHUNKS = 2


stencil_coef = (-205.0 / 72.0, 8.0 / 5.0, -1.0 / 5.0, 8.0 / 315.0, -1.0 / 560.0)
stencil_reach = 4
center = 5.25
half = 4.75


def extended(array, sides, width):
    for axis, dim in sides:
        count, length = (lax.axis_size(axis), array.shape[dim])
        up = [(i, (i + 1) % count) for i in range(count)]
        down = [(j, i) for i, j in up]
        last = lax.slice_in_dim(array, length - width, length, axis=dim)
        initial = lax.slice_in_dim(array, 0, width, axis=dim)
        before = lax.ppermute(last, axis, up)
        after = lax.ppermute(initial, axis, down)
        array = jnp.concatenate([before, array, after], axis=dim)
    return array


def hp_dot(left, right, dims):
    return lax.dot_general(
        left,
        right,
        (dims, ((), ())),
        precision=lax.Precision.HIGHEST,
        preferred_element_type=jnp.float32,
    )


def hamiltonian(field, padded, potential):
    depth = field.shape[1]
    laplace = 3.0 * stencil_coef[0] * field
    for reach in range(1, 5):
        near = (
            padded[:, stencil_reach + reach : stencil_reach + reach + depth]
            + padded[:, stencil_reach - reach : stencil_reach - reach + depth]
        )
        near = near + jnp.roll(field, reach, 2) + jnp.roll(field, -reach, 2)
        near = near + jnp.roll(field, reach, 3) + jnp.roll(field, -reach, 3)
        laplace = laplace + stencil_coef[reach] * near
    return potential[None] * field - 0.5 * laplace


def group_sum(x, axis, stride, size):
    count = lax.axis_size(axis)
    pos = (lax.axis_index(axis) // stride) % size
    received = [x]
    for shift in range(1, size):
        pairs = []
        for i in range(count):
            p = (i // stride) % size
            pairs.append((i, i + (((p + shift) % size) - p) * stride))
        received.append(lax.ppermute(x, axis, pairs))
    def at(p):
        value = received[0]
        for shift in range(1, size):
            value = jnp.where((pos - p) % size == shift, received[shift], value)
        return value
    values = [at(p) for p in range(size)]
    while len(values) > 1:
        values = [values[i] + values[i + 1] for i in range(0, len(values), 2)]
    return values[0]


def mesh_sum(x):
    x = group_sum(x, "dom", 1, lax.axis_size("dom"))
    x = group_sum(x, "band", 1, 4)
    return group_sum(x, "band", 4, lax.axis_size("band") // 4)


def gram_kernel(rows, f_ref, h_ref, c_ref, g_ref):
    nb = c_ref.shape[0]
    c_ref[...] = jnp.zeros_like(c_ref)
    g_ref[...] = jnp.zeros_like(g_ref)
    for r in range(rows):
        f = f_ref[pl.ds(r, nb, stride=rows), :]
        h = h_ref[pl.ds(r, nb, stride=rows), :]
        c_ref[...] += hp_dot(f, f, ((1,), (1,)))
        g_ref[...] += hp_dot(f, h, ((1,), (1,)))


def rotate_kernel(rows, m_ref, f_ref, o_ref):
    nb = m_ref.shape[0]
    for r in range(rows):
        o_ref[pl.ds(r, nb, stride=rows), :] = hp_dot(
            m_ref[...], f_ref[pl.ds(r, nb, stride=rows), :], ((1,), (0,))
        )


def inverse_kernel(c_ref, o_ref, a_ref, b_ref):
    n = c_ref.shape[0]
    a_ref[...] = jnp.zeros_like(a_ref)
    a_ref[:, :n] = c_ref[...]
    shape = a_ref.shape
    sub = lax.broadcasted_iota(jnp.int32, shape, 0)
    lane = lax.broadcasted_iota(jnp.int32, shape, 1)
    b_ref[...] = jnp.where(sub == lane, 1.0, 0.0).astype(jnp.float32)
    tile = 128
    tiles = shape[1] // tile

    def segment(k0, k1, r0):
        ta, tb = k0 // tile, (k1 - 1) // tile + 1
        rows = shape[0] - r0

        def step(k, carry):
            row_a = a_ref[pl.ds(k, 1), :][:, ta * tile :]
            row_b = b_ref[pl.ds(k, 1), :][:, : tb * tile]
            a = a_ref[r0:, ta * tile :]
            lane_a = lax.broadcasted_iota(jnp.int32, a.shape, 1) + ta * tile
            pivot = jnp.sum(jnp.where(lane_a[:1] == k, row_a, 0.0), axis=1, keepdims=True)
            col = jnp.sum(jnp.where(lane_a == k, a, 0.0), axis=1, keepdims=True)
            below = lax.broadcasted_iota(jnp.int32, (rows, 1), 0) + r0 > k
            factor = jnp.where(below, col, 0.0) * (1.0 / pivot)
            a_ref[r0:, ta * tile :] = a - factor * row_a
            b_ref[r0:, : tb * tile] = b_ref[r0:, : tb * tile] - factor * row_b
            return carry

        lax.fori_loop(k0, k1, step, 0)

    bounds = sorted({0, n} | {t * tile for t in range(1, tiles) if t * tile < n})
    for k0, k1 in zip(bounds[:-1], bounds[1:]):
        segment(k0, k1, (k0 // 8) * 8)
    a = a_ref[...]
    diag = jnp.sum(jnp.where(sub == lane, a, 0.0), axis=1, keepdims=True)
    o_ref[...] = (b_ref[...] / jnp.sqrt(diag))[:, :n]


def lower_inverse(c):
    n = c.shape[0]
    wide = ((n + 127) // 128) * 128
    return pl.pallas_call(
        inverse_kernel,
        out_shape=jax.ShapeDtypeStruct((n, n), jnp.float32),
        in_specs=[vspec()],
        out_specs=vspec(),
        scratch_shapes=[pltpu.VMEM((n, wide), jnp.float32), pltpu.VMEM((n, wide), jnp.float32)],
    )(c)


def vspec():
    return pl.BlockSpec(memory_space=pltpu.VMEM)


def grams(rows, f, h):
    nb = f.shape[0] // rows
    out = jax.ShapeDtypeStruct((nb, nb), jnp.float32)
    return pl.pallas_call(
        lambda *refs: gram_kernel(rows, *refs),
        out_shape=(out, out),
        in_specs=[vspec(), vspec()],
        out_specs=(vspec(), vspec()),
    )(f, h)


def rotate(rows, m, f):
    return pl.pallas_call(
        lambda *refs: rotate_kernel(rows, *refs),
        out_shape=jax.ShapeDtypeStruct(f.shape, jnp.float32),
        in_specs=[vspec(), vspec()],
        out_specs=vspec(),
    )(m, f)


def local(psi, potential):
    bdev = psi.shape[0]
    depth, rows_y, rows_x = (psi.shape[1], psi.shape[2], psi.shape[3])
    nbands = bdev * lax.axis_size("band")
    ncells = depth * lax.axis_size("dom") * rows_y * rows_x
    own_start = lax.axis_index("band") * bdev

    def apply(field):
        padded = extended(field, (("dom", 1),), stencil_reach)
        return hamiltonian(field, padded, potential)

    chunks = CHUNKS if bdev % CHUNKS == 0 else 1
    width = bdev // chunks
    previous = [psi[i * width : (i + 1) * width] for i in range(chunks)]
    current = [(apply(p) - center * p) / half for p in previous]
    for order in range(1, DEGREE):
        following = [2.0 / half * (apply(c) - center * c) - p for c, p in zip(current, previous)]
        previous, current = (current, following)
    image = jnp.concatenate([apply(c) for c in current])
    current = jnp.concatenate(current)
    groups = lax.axis_size("band")
    rows = depth * rows_y * rows_x // groups // rows_x
    lanes = rows_x
    chunked = jnp.stack([current, image]).reshape(2, bdev, groups, rows, lanes)
    spread = lax.all_to_all(chunked, "band", 2, 2, tiled=True)
    flat_cd = spread[0].reshape(bdev * groups * rows, lanes)
    image_cd = spread[1].reshape(bdev * groups * rows, lanes)
    c_perm, g_perm = grams(rows, flat_cd, image_cd)
    below = lax.broadcasted_iota(jnp.int32, (nbands, nbands), 0) >= lax.broadcasted_iota(
        jnp.int32, (nbands, nbands), 1
    )
    packed = jnp.concatenate(
        [jnp.where(below, c_perm, g_perm), jnp.sum(jnp.where(lax.broadcasted_iota(jnp.int32, (nbands, nbands), 0) == lax.broadcasted_iota(jnp.int32, (nbands, nbands), 1), g_perm, 0.0), axis=0, keepdims=True), jnp.zeros((7, nbands), jnp.float32)]
    )
    packed = mesh_sum(packed) / ncells
    tri, g_diag = packed[:nbands], packed[nbands]
    c_sum = jnp.where(below, tri, tri.T)
    g_sum = jnp.where(below, tri.T, tri)
    g_sum = jnp.where(jnp.eye(nbands, dtype=bool), g_diag[None, :], g_sum)

    def to_true(m):
        return m.reshape(bdev, groups, bdev, groups).transpose(1, 0, 3, 2).reshape(nbands, nbands)

    def to_perm(m):
        return m.reshape(groups, bdev, groups, bdev).transpose(1, 0, 3, 2).reshape(nbands, nbands)

    correlation, gram = to_true(c_sum), to_true(g_sum)
    inverse = lower_inverse(correlation)
    basis_cd = rotate(rows, to_perm(inverse), flat_cd).reshape(bdev, groups, rows, lanes)
    basis = lax.all_to_all(basis_cd, "band", 1, 1, tiled=True).reshape(psi.shape)
    own_rows = lax.dynamic_slice_in_dim(inverse, own_start, bdev, 0)
    projected = hp_dot(hp_dot(own_rows, gram, ((1,), (0,))), inverse, ((1,), (1,)))
    return (basis, projected)


def solution(mesh):
    in_specs = (P("band", "dom", None, None), P("dom", None, None))
    out_specs = (P("band", "dom", None, None), P("band", None))
    return jax.shard_map(local, mesh=mesh, in_specs=in_specs, out_specs=out_specs, check_vma=False)
```

```python
import jax
import jax.numpy as jnp
from jax import lax
from jax.experimental import pallas as pl
from jax.experimental.pallas import tpu as pltpu
from jax.sharding import PartitionSpec as P

DEGREE = 4
CHUNKS = 2


stencil_coef = (-205.0 / 72.0, 8.0 / 5.0, -1.0 / 5.0, 8.0 / 315.0, -1.0 / 560.0)
stencil_reach = 4
center = 5.25
half = 4.75


def extended(array, sides, width):
    for axis, dim in sides:
        count, length = (lax.axis_size(axis), array.shape[dim])
        up = [(i, (i + 1) % count) for i in range(count)]
        down = [(j, i) for i, j in up]
        last = lax.slice_in_dim(array, length - width, length, axis=dim)
        initial = lax.slice_in_dim(array, 0, width, axis=dim)
        before = lax.ppermute(last, axis, up)
        after = lax.ppermute(initial, axis, down)
        array = jnp.concatenate([before, array, after], axis=dim)
    return array


def hp_dot(left, right, dims):
    return lax.dot_general(
        left,
        right,
        (dims, ((), ())),
        precision=lax.Precision.HIGHEST,
        preferred_element_type=jnp.float32,
    )


def hamiltonian(field, padded, potential):
    depth = field.shape[1]
    laplace = 3.0 * stencil_coef[0] * field
    for reach in range(1, 5):
        near = (
            padded[:, stencil_reach + reach : stencil_reach + reach + depth]
            + padded[:, stencil_reach - reach : stencil_reach - reach + depth]
        )
        near = near + jnp.roll(field, reach, 2) + jnp.roll(field, -reach, 2)
        near = near + jnp.roll(field, reach, 3) + jnp.roll(field, -reach, 3)
        laplace = laplace + stencil_coef[reach] * near
    return potential[None] * field - 0.5 * laplace


def group_sum(x, axis, stride, size):
    count = lax.axis_size(axis)
    pos = (lax.axis_index(axis) // stride) % size
    received = [x]
    for shift in range(1, size):
        pairs = []
        for i in range(count):
            p = (i // stride) % size
            pairs.append((i, i + (((p + shift) % size) - p) * stride))
        received.append(lax.ppermute(x, axis, pairs))
    def at(p):
        value = received[0]
        for shift in range(1, size):
            value = jnp.where((pos - p) % size == shift, received[shift], value)
        return value
    values = [at(p) for p in range(size)]
    while len(values) > 1:
        values = [values[i] + values[i + 1] for i in range(0, len(values), 2)]
    return values[0]


def mesh_sum(x):
    x = group_sum(x, "dom", 1, 2)
    x = group_sum(x, "dom", 2, lax.axis_size("dom") // 2)
    x = group_sum(x, "band", 1, 4)
    return group_sum(x, "band", 4, lax.axis_size("band") // 4)


def gram_kernel(rows, f_ref, h_ref, c_ref, g_ref):
    nb = c_ref.shape[0]
    c_ref[...] = jnp.zeros_like(c_ref)
    g_ref[...] = jnp.zeros_like(g_ref)
    for r in range(rows):
        f = f_ref[pl.ds(r, nb, stride=rows), :]
        h = h_ref[pl.ds(r, nb, stride=rows), :]
        c_ref[...] += hp_dot(f, f, ((1,), (1,)))
        g_ref[...] += hp_dot(f, h, ((1,), (1,)))


def rotate_kernel(rows, m_ref, f_ref, o_ref):
    nb = m_ref.shape[0]
    for r in range(rows):
        o_ref[pl.ds(r, nb, stride=rows), :] = hp_dot(
            m_ref[...], f_ref[pl.ds(r, nb, stride=rows), :], ((1,), (0,))
        )


def inverse_kernel(c_ref, o_ref, a_ref, b_ref):
    n = c_ref.shape[0]
    a_ref[...] = jnp.zeros_like(a_ref)
    a_ref[:, :n] = c_ref[...]
    shape = a_ref.shape
    sub = lax.broadcasted_iota(jnp.int32, shape, 0)
    lane = lax.broadcasted_iota(jnp.int32, shape, 1)
    b_ref[...] = jnp.where(sub == lane, 1.0, 0.0).astype(jnp.float32)
    tile = 128
    tiles = shape[1] // tile

    def segment(k0, k1, r0):
        ta, tb = k0 // tile, (k1 - 1) // tile + 1
        rows = shape[0] - r0

        def step(k, carry):
            row_a = a_ref[pl.ds(k, 1), :][:, ta * tile :]
            row_b = b_ref[pl.ds(k, 1), :][:, : tb * tile]
            a = a_ref[r0:, ta * tile :]
            lane_a = lax.broadcasted_iota(jnp.int32, a.shape, 1) + ta * tile
            pivot = jnp.sum(jnp.where(lane_a[:1] == k, row_a, 0.0), axis=1, keepdims=True)
            col = jnp.sum(jnp.where(lane_a == k, a, 0.0), axis=1, keepdims=True)
            below = lax.broadcasted_iota(jnp.int32, (rows, 1), 0) + r0 > k
            factor = jnp.where(below, col, 0.0) * (1.0 / pivot)
            a_ref[r0:, ta * tile :] = a - factor * row_a
            b_ref[r0:, : tb * tile] = b_ref[r0:, : tb * tile] - factor * row_b
            return carry

        lax.fori_loop(k0, k1, step, 0, unroll=4)

    bounds = sorted({0, n} | {t * tile for t in range(1, tiles) if t * tile < n})
    for k0, k1 in zip(bounds[:-1], bounds[1:]):
        segment(k0, k1, (k0 // 8) * 8)
    a = a_ref[...]
    diag = jnp.sum(jnp.where(sub == lane, a, 0.0), axis=1, keepdims=True)
    o_ref[...] = (b_ref[...] / jnp.sqrt(diag))[:, :n]


def lower_inverse(c):
    n = c.shape[0]
    wide = ((n + 127) // 128) * 128
    return pl.pallas_call(
        inverse_kernel,
        out_shape=jax.ShapeDtypeStruct((n, n), jnp.float32),
        in_specs=[vspec()],
        out_specs=vspec(),
        scratch_shapes=[pltpu.VMEM((n, wide), jnp.float32), pltpu.VMEM((n, wide), jnp.float32)],
    )(c)


def vspec():
    return pl.BlockSpec(memory_space=pltpu.VMEM)


def grams(rows, f, h):
    nb = f.shape[0] // rows
    out = jax.ShapeDtypeStruct((nb, nb), jnp.float32)
    return pl.pallas_call(
        lambda *refs: gram_kernel(rows, *refs),
        out_shape=(out, out),
        in_specs=[vspec(), vspec()],
        out_specs=(vspec(), vspec()),
    )(f, h)


def rotate(rows, m, f):
    return pl.pallas_call(
        lambda *refs: rotate_kernel(rows, *refs),
        out_shape=jax.ShapeDtypeStruct(f.shape, jnp.float32),
        in_specs=[vspec(), vspec()],
        out_specs=vspec(),
    )(m, f)


def local(psi, potential):
    bdev = psi.shape[0]
    depth, rows_y, rows_x = (psi.shape[1], psi.shape[2], psi.shape[3])
    nbands = bdev * lax.axis_size("band")
    ncells = depth * lax.axis_size("dom") * rows_y * rows_x
    own_start = lax.axis_index("band") * bdev

    def apply(field):
        padded = extended(field, (("dom", 1),), stencil_reach)
        return hamiltonian(field, padded, potential)

    chunks = CHUNKS if bdev % CHUNKS == 0 else 1
    width = bdev // chunks
    previous = [psi[i * width : (i + 1) * width] for i in range(chunks)]
    current = [(apply(p) - center * p) / half for p in previous]
    for order in range(1, DEGREE):
        following = [2.0 / half * (apply(c) - center * c) - p for c, p in zip(current, previous)]
        previous, current = (current, following)
    image = jnp.concatenate([apply(c) for c in current])
    current = jnp.concatenate(current)
    groups = lax.axis_size("band")
    rows = depth * rows_y * rows_x // groups // rows_x
    lanes = rows_x
    chunked = jnp.stack([current, image]).reshape(2, bdev, groups, rows, lanes)
    spread = lax.all_to_all(chunked, "band", 2, 2, tiled=True)
    flat_cd = spread[0].reshape(bdev * groups * rows, lanes)
    image_cd = spread[1].reshape(bdev * groups * rows, lanes)
    c_perm, g_perm = grams(rows, flat_cd, image_cd)
    below = lax.broadcasted_iota(jnp.int32, (nbands, nbands), 0) >= lax.broadcasted_iota(
        jnp.int32, (nbands, nbands), 1
    )
    packed = jnp.concatenate(
        [jnp.where(below, c_perm, g_perm), jnp.sum(jnp.where(lax.broadcasted_iota(jnp.int32, (nbands, nbands), 0) == lax.broadcasted_iota(jnp.int32, (nbands, nbands), 1), g_perm, 0.0), axis=0, keepdims=True), jnp.zeros((7, nbands), jnp.float32)]
    )
    packed = mesh_sum(packed) / ncells
    tri, g_diag = packed[:nbands], packed[nbands]
    c_sum = jnp.where(below, tri, tri.T)
    g_sum = jnp.where(below, tri.T, tri)
    g_sum = jnp.where(jnp.eye(nbands, dtype=bool), g_diag[None, :], g_sum)

    def to_true(m):
        return m.reshape(bdev, groups, bdev, groups).transpose(1, 0, 3, 2).reshape(nbands, nbands)

    def to_perm(m):
        return m.reshape(groups, bdev, groups, bdev).transpose(1, 0, 3, 2).reshape(nbands, nbands)

    correlation, gram = to_true(c_sum), to_true(g_sum)
    inverse = lower_inverse(correlation)
    basis_cd = rotate(rows, to_perm(inverse), flat_cd).reshape(bdev, groups, rows, lanes)
    basis = lax.all_to_all(basis_cd, "band", 1, 1, tiled=True).reshape(psi.shape)
    own_rows = lax.dynamic_slice_in_dim(inverse, own_start, bdev, 0)
    projected = hp_dot(hp_dot(own_rows, gram, ((1,), (0,))), inverse, ((1,), (1,)))
    return (basis, projected)


def solution(mesh):
    in_specs = (P("band", "dom", None, None), P("dom", None, None))
    out_specs = (P("band", "dom", None, None), P("band", None))
    return jax.shard_map(local, mesh=mesh, in_specs=in_specs, out_specs=out_specs, check_vma=False)
```

```python
import jax
import jax.numpy as jnp
from jax import lax
from jax.experimental import pallas as pl
from jax.experimental.pallas import tpu as pltpu
from jax.sharding import PartitionSpec as P

DEGREE = 4
CHUNKS = 2


stencil_coef = (-205.0 / 72.0, 8.0 / 5.0, -1.0 / 5.0, 8.0 / 315.0, -1.0 / 560.0)
stencil_reach = 4
center = 5.25
half = 4.75


def extended(array, sides, width):
    for axis, dim in sides:
        count, length = (lax.axis_size(axis), array.shape[dim])
        up = [(i, (i + 1) % count) for i in range(count)]
        down = [(j, i) for i, j in up]
        last = lax.slice_in_dim(array, length - width, length, axis=dim)
        initial = lax.slice_in_dim(array, 0, width, axis=dim)
        before = lax.ppermute(last, axis, up)
        after = lax.ppermute(initial, axis, down)
        array = jnp.concatenate([before, array, after], axis=dim)
    return array


def hp_dot(left, right, dims):
    return lax.dot_general(
        left,
        right,
        (dims, ((), ())),
        precision=lax.Precision.HIGHEST,
        preferred_element_type=jnp.float32,
    )


def hamiltonian(field, padded, potential):
    depth = field.shape[1]
    laplace = 3.0 * stencil_coef[0] * field
    for reach in range(1, 5):
        near = (
            padded[:, stencil_reach + reach : stencil_reach + reach + depth]
            + padded[:, stencil_reach - reach : stencil_reach - reach + depth]
        )
        near = near + jnp.roll(field, reach, 2) + jnp.roll(field, -reach, 2)
        near = near + jnp.roll(field, reach, 3) + jnp.roll(field, -reach, 3)
        laplace = laplace + stencil_coef[reach] * near
    return potential[None] * field - 0.5 * laplace


def group_sum(x, axis, stride, size):
    count = lax.axis_size(axis)
    pos = (lax.axis_index(axis) // stride) % size
    received = [x]
    for shift in range(1, size):
        pairs = []
        for i in range(count):
            p = (i // stride) % size
            pairs.append((i, i + (((p + shift) % size) - p) * stride))
        received.append(lax.ppermute(x, axis, pairs))
    def at(p):
        value = received[0]
        for shift in range(1, size):
            value = jnp.where((pos - p) % size == shift, received[shift], value)
        return value
    values = [at(p) for p in range(size)]
    while len(values) > 1:
        values = [values[i] + values[i + 1] for i in range(0, len(values), 2)]
    return values[0]


def mesh_sum(x):
    x = group_sum(x, "band", 1, 4)
    x = group_sum(x, "band", 4, lax.axis_size("band") // 4)
    x = group_sum(x, "dom", 1, 2)
    return group_sum(x, "dom", 2, lax.axis_size("dom") // 2)


def gram_kernel(rows, f_ref, h_ref, c_ref, g_ref):
    nb = c_ref.shape[0]
    c_ref[...] = jnp.zeros_like(c_ref)
    g_ref[...] = jnp.zeros_like(g_ref)
    for r in range(rows):
        f = f_ref[pl.ds(r, nb, stride=rows), :]
        h = h_ref[pl.ds(r, nb, stride=rows), :]
        c_ref[...] += hp_dot(f, f, ((1,), (1,)))
        g_ref[...] += hp_dot(f, h, ((1,), (1,)))


def rotate_kernel(rows, m_ref, f_ref, o_ref):
    nb = m_ref.shape[0]
    for r in range(rows):
        o_ref[pl.ds(r, nb, stride=rows), :] = hp_dot(
            m_ref[...], f_ref[pl.ds(r, nb, stride=rows), :], ((1,), (0,))
        )


def inverse_kernel(c_ref, o_ref, a_ref, b_ref):
    n = c_ref.shape[0]
    a_ref[...] = jnp.zeros_like(a_ref)
    a_ref[:, :n] = c_ref[...]
    shape = a_ref.shape
    sub = lax.broadcasted_iota(jnp.int32, shape, 0)
    lane = lax.broadcasted_iota(jnp.int32, shape, 1)
    b_ref[...] = jnp.where(sub == lane, 1.0, 0.0).astype(jnp.float32)
    tile = 128
    tiles = shape[1] // tile

    def segment(k0, k1, r0):
        ta, tb = k0 // tile, (k1 - 1) // tile + 1
        rows = shape[0] - r0

        def step(k, carry):
            row_a = a_ref[pl.ds(k, 1), :][:, ta * tile :]
            row_b = b_ref[pl.ds(k, 1), :][:, : tb * tile]
            a = a_ref[r0:, ta * tile :]
            lane_a = lax.broadcasted_iota(jnp.int32, a.shape, 1) + ta * tile
            pivot = jnp.sum(jnp.where(lane_a[:1] == k, row_a, 0.0), axis=1, keepdims=True)
            col = jnp.sum(jnp.where(lane_a == k, a, 0.0), axis=1, keepdims=True)
            below = lax.broadcasted_iota(jnp.int32, (rows, 1), 0) + r0 > k
            factor = jnp.where(below, col, 0.0) * (1.0 / pivot)
            a_ref[r0:, ta * tile :] = a - factor * row_a
            b_ref[r0:, : tb * tile] = b_ref[r0:, : tb * tile] - factor * row_b
            return carry

        lax.fori_loop(k0, k1, step, 0)

    bounds = sorted({0, n} | {t * tile for t in range(1, tiles) if t * tile < n})
    for k0, k1 in zip(bounds[:-1], bounds[1:]):
        segment(k0, k1, (k0 // 8) * 8)
    a = a_ref[...]
    diag = jnp.sum(jnp.where(sub == lane, a, 0.0), axis=1, keepdims=True)
    o_ref[...] = (b_ref[...] / jnp.sqrt(diag))[:, :n]


def lower_inverse(c):
    n = c.shape[0]
    wide = ((n + 127) // 128) * 128
    return pl.pallas_call(
        inverse_kernel,
        out_shape=jax.ShapeDtypeStruct((n, n), jnp.float32),
        in_specs=[vspec()],
        out_specs=vspec(),
        scratch_shapes=[pltpu.VMEM((n, wide), jnp.float32), pltpu.VMEM((n, wide), jnp.float32)],
    )(c)


def vspec():
    return pl.BlockSpec(memory_space=pltpu.VMEM)


def grams(rows, f, h):
    nb = f.shape[0] // rows
    out = jax.ShapeDtypeStruct((nb, nb), jnp.float32)
    return pl.pallas_call(
        lambda *refs: gram_kernel(rows, *refs),
        out_shape=(out, out),
        in_specs=[vspec(), vspec()],
        out_specs=(vspec(), vspec()),
    )(f, h)


def rotate(rows, m, f):
    return pl.pallas_call(
        lambda *refs: rotate_kernel(rows, *refs),
        out_shape=jax.ShapeDtypeStruct(f.shape, jnp.float32),
        in_specs=[vspec(), vspec()],
        out_specs=vspec(),
    )(m, f)


def local(psi, potential):
    bdev = psi.shape[0]
    depth, rows_y, rows_x = (psi.shape[1], psi.shape[2], psi.shape[3])
    nbands = bdev * lax.axis_size("band")
    ncells = depth * lax.axis_size("dom") * rows_y * rows_x
    own_start = lax.axis_index("band") * bdev

    def apply(field):
        padded = extended(field, (("dom", 1),), stencil_reach)
        return hamiltonian(field, padded, potential)

    chunks = CHUNKS if bdev % CHUNKS == 0 else 1
    width = bdev // chunks
    previous = [psi[i * width : (i + 1) * width] for i in range(chunks)]
    current = [(apply(p) - center * p) / half for p in previous]
    for order in range(1, DEGREE):
        following = [2.0 / half * (apply(c) - center * c) - p for c, p in zip(current, previous)]
        previous, current = (current, following)
    image = jnp.concatenate([apply(c) for c in current])
    current = jnp.concatenate(current)
    groups = lax.axis_size("band")
    rows = depth * rows_y * rows_x // groups // rows_x
    lanes = rows_x
    chunked = jnp.stack([current, image]).reshape(2, bdev, groups, rows, lanes)
    spread = lax.all_to_all(chunked, "band", 2, 2, tiled=True)
    flat_cd = spread[0].reshape(bdev * groups * rows, lanes)
    image_cd = spread[1].reshape(bdev * groups * rows, lanes)
    c_perm, g_perm = grams(rows, flat_cd, image_cd)
    below = lax.broadcasted_iota(jnp.int32, (nbands, nbands), 0) >= lax.broadcasted_iota(
        jnp.int32, (nbands, nbands), 1
    )
    packed = jnp.concatenate(
        [jnp.where(below, c_perm, g_perm), jnp.sum(jnp.where(lax.broadcasted_iota(jnp.int32, (nbands, nbands), 0) == lax.broadcasted_iota(jnp.int32, (nbands, nbands), 1), g_perm, 0.0), axis=0, keepdims=True), jnp.zeros((7, nbands), jnp.float32)]
    )
    packed = mesh_sum(packed) / ncells
    tri, g_diag = packed[:nbands], packed[nbands]
    c_sum = jnp.where(below, tri, tri.T)
    g_sum = jnp.where(below, tri.T, tri)
    g_sum = jnp.where(jnp.eye(nbands, dtype=bool), g_diag[None, :], g_sum)

    def to_true(m):
        return m.reshape(bdev, groups, bdev, groups).transpose(1, 0, 3, 2).reshape(nbands, nbands)

    def to_perm(m):
        return m.reshape(groups, bdev, groups, bdev).transpose(1, 0, 3, 2).reshape(nbands, nbands)

    correlation, gram = to_true(c_sum), to_true(g_sum)
    inverse = lower_inverse(correlation)
    basis_cd = rotate(rows, to_perm(inverse), flat_cd).reshape(bdev, groups, rows, lanes)
    basis = lax.all_to_all(basis_cd, "band", 1, 1, tiled=True).reshape(psi.shape)
    own_rows = lax.dynamic_slice_in_dim(inverse, own_start, bdev, 0)
    projected = hp_dot(hp_dot(own_rows, gram, ((1,), (0,))), inverse, ((1,), (1,)))
    return (basis, projected)


def solution(mesh):
    in_specs = (P("band", "dom", None, None), P("dom", None, None))
    out_specs = (P("band", "dom", None, None), P("band", None))
    return jax.shard_map(local, mesh=mesh, in_specs=in_specs, out_specs=out_specs, check_vma=False)
```

```python
import jax
import jax.numpy as jnp
from jax import lax
from jax.experimental import pallas as pl
from jax.experimental.pallas import tpu as pltpu
from jax.sharding import PartitionSpec as P

DEGREE = 4
CHUNKS = 2


stencil_coef = (-205.0 / 72.0, 8.0 / 5.0, -1.0 / 5.0, 8.0 / 315.0, -1.0 / 560.0)
stencil_reach = 4
center = 5.25
half = 4.75


def extended(array, sides, width):
    for axis, dim in sides:
        count, length = (lax.axis_size(axis), array.shape[dim])
        up = [(i, (i + 1) % count) for i in range(count)]
        down = [(j, i) for i, j in up]
        last = lax.slice_in_dim(array, length - width, length, axis=dim)
        initial = lax.slice_in_dim(array, 0, width, axis=dim)
        before = lax.ppermute(last, axis, up)
        after = lax.ppermute(initial, axis, down)
        array = jnp.concatenate([before, array, after], axis=dim)
    return array


def hp_dot(left, right, dims):
    return lax.dot_general(
        left,
        right,
        (dims, ((), ())),
        precision=lax.Precision.HIGHEST,
        preferred_element_type=jnp.float32,
    )


def hamiltonian(field, padded, potential):
    depth = field.shape[1]
    laplace = 3.0 * stencil_coef[0] * field
    for reach in range(1, 5):
        near = (
            padded[:, stencil_reach + reach : stencil_reach + reach + depth]
            + padded[:, stencil_reach - reach : stencil_reach - reach + depth]
        )
        near = near + jnp.roll(field, reach, 2) + jnp.roll(field, -reach, 2)
        near = near + jnp.roll(field, reach, 3) + jnp.roll(field, -reach, 3)
        laplace = laplace + stencil_coef[reach] * near
    return potential[None] * field - 0.5 * laplace


def group_sum(x, axis, stride, size):
    count = lax.axis_size(axis)
    pos = (lax.axis_index(axis) // stride) % size
    received = [x]
    for shift in range(1, size):
        pairs = []
        for i in range(count):
            p = (i // stride) % size
            pairs.append((i, i + (((p + shift) % size) - p) * stride))
        received.append(lax.ppermute(x, axis, pairs))
    def at(p):
        value = received[0]
        for shift in range(1, size):
            value = jnp.where((pos - p) % size == shift, received[shift], value)
        return value
    values = [at(p) for p in range(size)]
    while len(values) > 1:
        values = [values[i] + values[i + 1] for i in range(0, len(values), 2)]
    return values[0]


def mesh_sum(x):
    x = group_sum(x, "band", 1, 4)
    x = group_sum(x, "band", 4, lax.axis_size("band") // 4)
    x = group_sum(x, "dom", 1, 2)
    return group_sum(x, "dom", 2, lax.axis_size("dom") // 2)


def gram_kernel(rows, f_ref, h_ref, c_ref, g_ref):
    nb = c_ref.shape[0]
    c_ref[...] = jnp.zeros_like(c_ref)
    g_ref[...] = jnp.zeros_like(g_ref)
    for r in range(rows):
        f = f_ref[pl.ds(r, nb, stride=rows), :]
        h = h_ref[pl.ds(r, nb, stride=rows), :]
        c_ref[...] += hp_dot(f, f, ((1,), (1,)))
        g_ref[...] += hp_dot(f, h, ((1,), (1,)))


def rotate_kernel(rows, m_ref, f_ref, o_ref):
    nb = m_ref.shape[0]
    for r in range(rows):
        o_ref[pl.ds(r, nb, stride=rows), :] = hp_dot(
            m_ref[...], f_ref[pl.ds(r, nb, stride=rows), :], ((1,), (0,))
        )


def inverse_kernel(c_ref, o_ref, a_ref, b_ref):
    n = c_ref.shape[0]
    a_ref[...] = jnp.zeros_like(a_ref)
    a_ref[:, :n] = c_ref[...]
    shape = a_ref.shape
    sub = lax.broadcasted_iota(jnp.int32, shape, 0)
    lane = lax.broadcasted_iota(jnp.int32, shape, 1)
    b_ref[...] = jnp.where(sub == lane, 1.0, 0.0).astype(jnp.float32)
    tile = 128
    tiles = shape[1] // tile

    def segment(k0, k1, r0):
        ta, tb = k0 // tile, (k1 - 1) // tile + 1
        rows = shape[0] - r0

        def step(k, carry):
            row_a = a_ref[pl.ds(k, 1), :][:, ta * tile :]
            row_b = b_ref[pl.ds(k, 1), :][:, : tb * tile]
            a = a_ref[r0:, ta * tile :]
            lane_a = lax.broadcasted_iota(jnp.int32, a.shape, 1) + ta * tile
            pivot = jnp.sum(jnp.where(lane_a[:1] == k, row_a, 0.0), axis=1, keepdims=True)
            col = jnp.sum(jnp.where(lane_a == k, a, 0.0), axis=1, keepdims=True)
            below = lax.broadcasted_iota(jnp.int32, (rows, 1), 0) + r0 > k
            factor = jnp.where(below, col, 0.0) * (1.0 / pivot)
            a_ref[r0:, ta * tile :] = a - factor * row_a
            b_ref[r0:, : tb * tile] = b_ref[r0:, : tb * tile] - factor * row_b
            return carry

        lax.fori_loop(k0, k1, step, 0)

    bounds = sorted({0, n} | {t * tile for t in range(1, tiles) if t * tile < n})
    for k0, k1 in zip(bounds[:-1], bounds[1:]):
        segment(k0, k1, (k0 // 8) * 8)
    a = a_ref[...]
    diag = jnp.sum(jnp.where(sub == lane, a, 0.0), axis=1, keepdims=True)
    o_ref[...] = (b_ref[...] / jnp.sqrt(diag))[:, :n]


def lower_inverse(c):
    n = c.shape[0]
    wide = ((n + 127) // 128) * 128
    return pl.pallas_call(
        inverse_kernel,
        out_shape=jax.ShapeDtypeStruct((n, n), jnp.float32),
        in_specs=[vspec()],
        out_specs=vspec(),
        scratch_shapes=[pltpu.VMEM((n, wide), jnp.float32), pltpu.VMEM((n, wide), jnp.float32)],
    )(c)


def vspec():
    return pl.BlockSpec(memory_space=pltpu.VMEM)


def grams(rows, f, h):
    nb = f.shape[0] // rows
    out = jax.ShapeDtypeStruct((nb, nb), jnp.float32)
    return pl.pallas_call(
        lambda *refs: gram_kernel(rows, *refs),
        out_shape=(out, out),
        in_specs=[vspec(), vspec()],
        out_specs=(vspec(), vspec()),
    )(f, h)


def rotate(rows, m, f):
    return pl.pallas_call(
        lambda *refs: rotate_kernel(rows, *refs),
        out_shape=jax.ShapeDtypeStruct(f.shape, jnp.float32),
        in_specs=[vspec(), vspec()],
        out_specs=vspec(),
    )(m, f)


def local(psi, potential):
    bdev = psi.shape[0]
    depth, rows_y, rows_x = (psi.shape[1], psi.shape[2], psi.shape[3])
    nbands = bdev * lax.axis_size("band")
    ncells = depth * lax.axis_size("dom") * rows_y * rows_x
    own_start = lax.axis_index("band") * bdev

    def apply(field):
        padded = extended(field, (("dom", 1),), stencil_reach)
        return hamiltonian(field, padded, potential)

    chunks = CHUNKS if bdev % CHUNKS == 0 else 1
    width = bdev // chunks
    previous = [psi[i * width : (i + 1) * width] for i in range(chunks)]
    current = [(apply(p) - center * p) / half for p in previous]
    for order in range(1, DEGREE):
        following = [2.0 / half * (apply(c) - center * c) - p for c, p in zip(current, previous)]
        previous, current = (current, following)
    image = jnp.concatenate([apply(c) for c in current])
    current = jnp.concatenate(current)
    groups = lax.axis_size("band")
    rows = depth * rows_y * rows_x // groups // rows_x
    lanes = rows_x
    chunked = jnp.stack([current, image]).reshape(2, bdev, groups, rows, lanes)
    spread = lax.all_to_all(chunked, "band", 2, 2, tiled=True)
    flat_cd = spread[0].reshape(bdev * groups * rows, lanes)
    image_cd = spread[1].reshape(bdev * groups * rows, lanes)
    c_perm, g_perm = grams(rows, flat_cd, image_cd)
    below = lax.broadcasted_iota(jnp.int32, (nbands, nbands), 0) >= lax.broadcasted_iota(
        jnp.int32, (nbands, nbands), 1
    )
    packed = jnp.concatenate(
        [jnp.where(below, c_perm, g_perm), jnp.sum(jnp.where(lax.broadcasted_iota(jnp.int32, (nbands, nbands), 0) == lax.broadcasted_iota(jnp.int32, (nbands, nbands), 1), g_perm, 0.0), axis=0, keepdims=True), jnp.zeros((7, nbands), jnp.float32)]
    )
    packed = mesh_sum(packed) / ncells
    tri, g_diag = packed[:nbands], packed[nbands]
    c_sum = jnp.where(below, tri, tri.T)
    g_sum = jnp.where(below, tri.T, tri)
    g_sum = jnp.where(jnp.eye(nbands, dtype=bool), g_diag[None, :], g_sum)

    def to_true(m):
        return m.reshape(bdev, groups, bdev, groups).transpose(1, 0, 3, 2).reshape(nbands, nbands)

    def to_perm(m):
        return m.reshape(groups, bdev, groups, bdev).transpose(1, 0, 3, 2).reshape(nbands, nbands)

    correlation, gram = to_true(c_sum), to_true(g_sum)
    inverse = lower_inverse(correlation)
    mixed = inverse.reshape(nbands, groups, bdev).transpose(0, 2, 1).reshape(nbands, nbands)
    basis_cd = rotate(rows, mixed, flat_cd).reshape(groups, bdev, rows, lanes)
    basis = lax.all_to_all(basis_cd, "band", 0, 0, tiled=True)
    basis = basis.transpose(1, 0, 2, 3).reshape(psi.shape)
    own_rows = lax.dynamic_slice_in_dim(inverse, own_start, bdev, 0)
    projected = hp_dot(hp_dot(own_rows, gram, ((1,), (0,))), inverse, ((1,), (1,)))
    return (basis, projected)


def solution(mesh):
    in_specs = (P("band", "dom", None, None), P("dom", None, None))
    out_specs = (P("band", "dom", None, None), P("band", None))
    return jax.shard_map(local, mesh=mesh, in_specs=in_specs, out_specs=out_specs, check_vma=False)
```

```python
import jax
import jax.numpy as jnp
from jax import lax
from jax.experimental import pallas as pl
from jax.experimental.pallas import tpu as pltpu
from jax.sharding import PartitionSpec as P

DEGREE = 4
CHUNKS = 2


stencil_coef = (-205.0 / 72.0, 8.0 / 5.0, -1.0 / 5.0, 8.0 / 315.0, -1.0 / 560.0)
stencil_reach = 4
center = 5.25
half = 4.75


def extended(array, sides, width):
    for axis, dim in sides:
        count, length = (lax.axis_size(axis), array.shape[dim])
        up = [(i, (i + 1) % count) for i in range(count)]
        down = [(j, i) for i, j in up]
        last = lax.slice_in_dim(array, length - width, length, axis=dim)
        initial = lax.slice_in_dim(array, 0, width, axis=dim)
        before = lax.ppermute(last, axis, up)
        after = lax.ppermute(initial, axis, down)
        array = jnp.concatenate([before, array, after], axis=dim)
    return array


def hp_dot(left, right, dims):
    return lax.dot_general(
        left,
        right,
        (dims, ((), ())),
        precision=lax.Precision.HIGHEST,
        preferred_element_type=jnp.float32,
    )


def hamiltonian(field, padded, potential):
    depth = field.shape[1]
    laplace = 3.0 * stencil_coef[0] * field
    for reach in range(1, 5):
        near = (
            padded[:, stencil_reach + reach : stencil_reach + reach + depth]
            + padded[:, stencil_reach - reach : stencil_reach - reach + depth]
        )
        near = near + jnp.roll(field, reach, 2) + jnp.roll(field, -reach, 2)
        near = near + jnp.roll(field, reach, 3) + jnp.roll(field, -reach, 3)
        laplace = laplace + stencil_coef[reach] * near
    return potential[None] * field - 0.5 * laplace


def group_sum(x, axis, stride, size):
    count = lax.axis_size(axis)
    pos = (lax.axis_index(axis) // stride) % size
    received = [x]
    for shift in range(1, size):
        pairs = []
        for i in range(count):
            p = (i // stride) % size
            pairs.append((i, i + (((p + shift) % size) - p) * stride))
        received.append(lax.ppermute(x, axis, pairs))
    def at(p):
        value = received[0]
        for shift in range(1, size):
            value = jnp.where((pos - p) % size == shift, received[shift], value)
        return value
    values = [at(p) for p in range(size)]
    while len(values) > 1:
        values = [values[i] + values[i + 1] for i in range(0, len(values), 2)]
    return values[0]


def mesh_sum(x):
    x = group_sum(x, "band", 1, 4)
    x = group_sum(x, "band", 4, lax.axis_size("band") // 4)
    x = group_sum(x, "dom", 1, 2)
    return group_sum(x, "dom", 2, lax.axis_size("dom") // 2)


def gram_kernel(rows, f_ref, h_ref, c_ref, g_ref):
    nb = c_ref.shape[0]
    c_ref[...] = jnp.zeros_like(c_ref)
    g_ref[...] = jnp.zeros_like(g_ref)
    for r in range(rows):
        f = f_ref[pl.ds(r, nb, stride=rows), :]
        h = h_ref[pl.ds(r, nb, stride=rows), :]
        c_ref[...] += hp_dot(f, f, ((1,), (1,)))
        g_ref[...] += hp_dot(f, h, ((1,), (1,)))


def rotate_kernel(rows, m_ref, f_ref, o_ref):
    nb = m_ref.shape[0]
    for r in range(rows):
        o_ref[pl.ds(r, nb, stride=rows), :] = hp_dot(
            m_ref[...], f_ref[pl.ds(r, nb, stride=rows), :], ((1,), (0,))
        )


def inverse_kernel(c_ref, o_ref, a_ref, b_ref):
    n = c_ref.shape[0]
    a_ref[...] = jnp.zeros_like(a_ref)
    a_ref[:, :n] = c_ref[...]
    shape = a_ref.shape
    sub = lax.broadcasted_iota(jnp.int32, shape, 0)
    lane = lax.broadcasted_iota(jnp.int32, shape, 1)
    b_ref[...] = jnp.where(sub == lane, 1.0, 0.0).astype(jnp.float32)
    tile = 128
    tiles = shape[1] // tile

    def segment(k0, k1, r0):
        ta, tb = k0 // tile, (k1 - 1) // tile + 1
        rows = shape[0] - r0

        def step(k, carry):
            row_a = a_ref[pl.ds(k, 1), :][:, ta * tile :]
            row_b = b_ref[pl.ds(k, 1), :][:, : tb * tile]
            a = a_ref[r0:, ta * tile :]
            lane_a = lax.broadcasted_iota(jnp.int32, a.shape, 1) + ta * tile
            pivot = jnp.sum(jnp.where(lane_a[:1] == k, row_a, 0.0), axis=1, keepdims=True)
            col = jnp.sum(jnp.where(lane_a == k, a, 0.0), axis=1, keepdims=True)
            below = lax.broadcasted_iota(jnp.int32, (rows, 1), 0) + r0 > k
            factor = jnp.where(below, col, 0.0) * (1.0 / pivot)
            a_ref[r0:, ta * tile :] = a - factor * row_a
            b_ref[r0:, : tb * tile] = b_ref[r0:, : tb * tile] - factor * row_b
            return carry

        lax.fori_loop(k0, k1, step, 0)

    bounds = sorted({0, n} | {t * tile for t in range(1, tiles) if t * tile < n})
    for k0, k1 in zip(bounds[:-1], bounds[1:]):
        segment(k0, k1, (k0 // 8) * 8)
    a = a_ref[...]
    diag = jnp.sum(jnp.where(sub == lane, a, 0.0), axis=1, keepdims=True)
    o_ref[...] = (b_ref[...] / jnp.sqrt(diag))[:, :n]


def lower_inverse(c):
    n = c.shape[0]
    wide = ((n + 127) // 128) * 128
    return pl.pallas_call(
        inverse_kernel,
        out_shape=jax.ShapeDtypeStruct((n, n), jnp.float32),
        in_specs=[vspec()],
        out_specs=vspec(),
        scratch_shapes=[pltpu.VMEM((n, wide), jnp.float32), pltpu.VMEM((n, wide), jnp.float32)],
    )(c)


def vspec():
    return pl.BlockSpec(memory_space=pltpu.VMEM)


def grams(rows, f, h):
    nb = f.shape[0] // rows
    out = jax.ShapeDtypeStruct((nb, nb), jnp.float32)
    return pl.pallas_call(
        lambda *refs: gram_kernel(rows, *refs),
        out_shape=(out, out),
        in_specs=[vspec(), vspec()],
        out_specs=(vspec(), vspec()),
    )(f, h)


def rotate(rows, m, f):
    return pl.pallas_call(
        lambda *refs: rotate_kernel(rows, *refs),
        out_shape=jax.ShapeDtypeStruct(f.shape, jnp.float32),
        in_specs=[vspec(), vspec()],
        out_specs=vspec(),
    )(m, f)


def local(psi, potential):
    bdev = psi.shape[0]
    depth, rows_y, rows_x = (psi.shape[1], psi.shape[2], psi.shape[3])
    nbands = bdev * lax.axis_size("band")
    ncells = depth * lax.axis_size("dom") * rows_y * rows_x
    own_start = lax.axis_index("band") * bdev

    def apply(field):
        padded = extended(field, (("dom", 1),), stencil_reach)
        return hamiltonian(field, padded, potential)

    chunks = CHUNKS if bdev % CHUNKS == 0 else 1
    width = bdev // chunks
    previous = [psi[i * width : (i + 1) * width] for i in range(chunks)]
    current = [(apply(p) - center * p) / half for p in previous]
    for order in range(1, DEGREE):
        following = [2.0 / half * (apply(c) - center * c) - p for c, p in zip(current, previous)]
        previous, current = (current, following)
    image = jnp.concatenate([apply(c) for c in current])
    current = jnp.concatenate(current)
    groups = lax.axis_size("band")
    rows = depth * rows_y * rows_x // groups // rows_x
    lanes = rows_x
    chunked = jnp.stack([current, image]).reshape(2, bdev, groups, rows, lanes).transpose(2, 0, 1, 3, 4)
    spread = lax.all_to_all(chunked, "band", 0, 0, tiled=True)
    flat_cd = spread[:, 0].reshape(bdev * groups * rows, lanes)
    image_cd = spread[:, 1].reshape(bdev * groups * rows, lanes)
    c_perm, g_perm = grams(rows, flat_cd, image_cd)
    below = lax.broadcasted_iota(jnp.int32, (nbands, nbands), 0) >= lax.broadcasted_iota(
        jnp.int32, (nbands, nbands), 1
    )
    packed = jnp.concatenate(
        [jnp.where(below, c_perm, g_perm), jnp.sum(jnp.where(lax.broadcasted_iota(jnp.int32, (nbands, nbands), 0) == lax.broadcasted_iota(jnp.int32, (nbands, nbands), 1), g_perm, 0.0), axis=0, keepdims=True), jnp.zeros((7, nbands), jnp.float32)]
    )
    packed = mesh_sum(packed) / ncells
    tri, g_diag = packed[:nbands], packed[nbands]
    c_sum = jnp.where(below, tri, tri.T)
    g_sum = jnp.where(below, tri.T, tri)
    g_sum = jnp.where(jnp.eye(nbands, dtype=bool), g_diag[None, :], g_sum)

    def to_true(m):
        return m.reshape(bdev, groups, bdev, groups).transpose(1, 0, 3, 2).reshape(nbands, nbands)

    def to_perm(m):
        return m.reshape(groups, bdev, groups, bdev).transpose(1, 0, 3, 2).reshape(nbands, nbands)

    correlation, gram = c_sum, g_sum
    inverse = lower_inverse(correlation)
    mixed = inverse
    basis_cd = rotate(rows, mixed, flat_cd).reshape(groups, bdev, rows, lanes)
    basis = lax.all_to_all(basis_cd, "band", 0, 0, tiled=True)
    basis = basis.transpose(1, 0, 2, 3).reshape(psi.shape)
    own_rows = lax.dynamic_slice_in_dim(inverse, own_start, bdev, 0)
    projected = hp_dot(hp_dot(own_rows, gram, ((1,), (0,))), inverse, ((1,), (1,)))
    return (basis, projected)


def solution(mesh):
    in_specs = (P("band", "dom", None, None), P("dom", None, None))
    out_specs = (P("band", "dom", None, None), P("band", None))
    return jax.shard_map(local, mesh=mesh, in_specs=in_specs, out_specs=out_specs, check_vma=False)
```
